512 devices in a mesh: segment: 8 (over z), gy: 64 (over x, y, core).
Axes of the slice: x: 4, y: 8, z: 8, core: 2. Of those that a mesh axis runs over, the one named last changes fastest.
Arguments:
- acts: bfloat16 [8, 8, 128, 32, 256], P('segment', None, 'gy'), may hold values from -6 to 6
- grad_out: bfloat16 [8, 128, 32, 256], P('segment', 'gy'), may hold values from -6 to 6
- w_plane: bfloat16 [8, 3, 3, 32, 32], P('segment'), may hold values from -0.375 to 0.375
- w_depth: bfloat16 [8, 3, 32, 32], P('segment'), may hold values from -0.625 to 0.625
- tiles: int32 [64, 12], P('gy'), may hold values from -1 to 15, as said below
Outputs:
- grad_in: bfloat16 [8, 128, 32, 256], P('segment', 'gy')
- grad_plane: float32 [8, 3, 3, 32, 32], P('segment')
- grad_depth: float32 [8, 3, 32, 32], P('segment')
The draws below stay inside these ranges and needn't reach their ends.
Inputs may be any that keep to these rules, and one draw needn't show every extreme that they name: Row s lists distinct tiles z * 2 + x-tile of slab s in its first entries and -1 after them; each row lists 1 to 12 tiles, and some row lists exactly 12.
All inputs are finite; a program needn't handle non-finite values.
Results may differ from the reference program's by a relative error of at most 0.02.
Values may be sent and summed in bfloat16 or wider, within the bound.
No kernel may reach another device: no remote copies, remote signals or barrier semaphores. Data moves between devices by JAX's collectives and lax.ppermute only.
A program may use at most 64 MiB of HBM per device.

```python
import jax
import jax.numpy as jnp

C = 32
Z = 8
Y_DEV = 2
TILE = 128
XT = 2
X = 256
NY = 128
SLABS = 64
LAYERS = 8
TILES = 16
CAP = 12


def draw_tiles(key, part):
    key_count, key_full, key_perm = jax.random.split(jax.random.fold_in(key, 7), 3)
    counts = jax.random.randint(key_count, (SLABS,), 1, CAP + 1)
    fullest = jax.random.randint(key_full, (), 0, SLABS)
    counts = jnp.where(jnp.arange(SLABS) == fullest, CAP, counts)
    slab_keys = jax.random.split(key_perm, SLABS)
    orders = jax.vmap(lambda one_key: jax.random.permutation(one_key, TILES))(slab_keys)[:, :CAP]
    listed = jnp.where(jnp.arange(CAP)[None, :] < counts[:, None], orders, -1)
    return listed.astype(jnp.int32)


def level_of(stream_key, dims, shards, smallest, largest):
    loudness = 1.0
    for position, blocks in shards:
        heights = jax.random.uniform(jax.random.fold_in(jax.random.fold_in(stream_key, 6), position), (blocks,), jnp.float32, smallest / len(shards), largest / len(shards))
        loudness = loudness * jnp.repeat(jnp.exp(heights), dims[position] // blocks).reshape((-1,) + (1,) * (len(dims) - 1 - position))
    return loudness


def scatter_about(rng, extent, scale, reach, pieces=(), kind=jnp.bfloat16):
    values = scale * jax.random.normal(rng, extent, jnp.float32)
    if pieces:
        values = values * level_of(rng, extent, pieces, -0.22, 0.18)
    return jnp.clip(values, -reach, reach).astype(kind)


def setup_inputs(seed: int = 0) -> dict:
    streams_of = jax.random.split(jax.random.key(seed), 6)
    return {
        "acts": scatter_about(streams_of[0], (LAYERS, Z, NY, C, X), 1.0, 6.0, ((0, 8), (2, 64))),
        "grad_out": scatter_about(streams_of[1], (Z, NY, C, X), 1.0, 6.0, ((0, 8), (1, 64))),
        "w_plane": scatter_about(streams_of[2], (LAYERS, 3, 3, C, C), (9 * C) ** -0.5, 0.375, ((0, 8),)),
        "w_depth": scatter_about(streams_of[3], (LAYERS, 3, C, C), (3 * C) ** -0.5, 0.625, ((0, 8),)),
        "tiles": draw_tiles(jax.random.fold_in(streams_of[5], 71), 0),
    }


def plane_conv(field, kernel):
    padded = jnp.pad(field.astype(jnp.float32), ((0, 0), (1, 1), (0, 0), (1, 1)))
    total = jnp.zeros(field.shape, jnp.float32)
    for i in range(3):
        for j in range(3):
            total = total + jnp.einsum('oc,zycx->zyox', kernel[i, j].astype(jnp.float32), padded[:, i:i + NY, :, j:j + X])
    return total

def plane_back(grad_mid, kernel):
    padded = jnp.pad(grad_mid.astype(jnp.float32), ((0, 0), (1, 1), (0, 0), (1, 1)))
    total = jnp.zeros(grad_mid.shape, jnp.float32)
    for i in range(3):
        for j in range(3):
            total = total + jnp.einsum('oc,zyox->zycx', kernel[i, j].astype(jnp.float32), padded[:, 2 - i:2 - i + NY, :, 2 - j:2 - j + X])
    return total

def plane_taps(grad_mid, field):
    padded = jnp.pad(field.astype(jnp.float32), ((0, 0), (1, 1), (0, 0), (1, 1)))
    gmid = grad_mid.astype(jnp.float32)
    rows_out = []
    for i in range(3):
        row_taps = []
        for j in range(3):
            row_taps.append(jnp.einsum('zyox,zycx->oc', gmid, padded[:, i:i + NY, :, j:j + X]))
        rows_out.append(jnp.stack(row_taps))
    return jnp.stack(rows_out)

def depth_pad(field):
    return jnp.pad(field.astype(jnp.float32), ((1, 1), (0, 0), (0, 0), (0, 0)))

def reference(acts, grad_out, w_plane, w_depth, tiles):
    hit = jnp.any(tiles[:, :, None] == jnp.arange(TILES, dtype=jnp.int32)[None, None, :], axis=1)
    mask = hit.astype(jnp.float32).reshape(SLABS, Z, XT).transpose(1, 0, 2)
    mask = jnp.repeat(jnp.repeat(mask, Y_DEV, axis=1), TILE, axis=2)[:, :, None, :]
    scale = 1.0 / jnp.sqrt(jnp.float32(Z * NY * X))
    grad = grad_out
    plane_list = []
    depth_list = []
    for layer in reversed(range(LAYERS)):
        field = acts[layer]
        mid = plane_conv(field, w_plane[layer]).astype(jnp.bfloat16)
        deep = depth_pad(mid)
        value = jnp.zeros(mid.shape, jnp.float32)
        for k in range(3):
            value = value + jnp.einsum('oc,zycx->zyox', w_depth[layer, k].astype(jnp.float32), deep[k:k + Z])
        sig = jax.nn.sigmoid(value)
        grad_mix = (mask * grad.astype(jnp.float32) * sig * (1.0 + value * (1.0 - sig))).astype(jnp.bfloat16)
        mix_deep = depth_pad(grad_mix)
        grad_mid = jnp.zeros(mid.shape, jnp.float32)
        depth_taps = []
        for k in range(3):
            grad_mid = grad_mid + jnp.einsum('oc,zyox->zycx', w_depth[layer, k].astype(jnp.float32), mix_deep[2 - k:2 - k + Z])
            depth_taps.append(jnp.einsum('zyox,zycx->oc', grad_mix.astype(jnp.float32), deep[k:k + Z]))
        grad_mid = grad_mid.astype(jnp.bfloat16)
        depth_list.insert(0, jnp.stack(depth_taps) * scale)
        plane_list.insert(0, plane_taps(grad_mid, field) * scale)
        grad = (grad.astype(jnp.float32) + plane_back(grad_mid, w_plane[layer])).astype(jnp.bfloat16)
    return (grad, jnp.stack(plane_list), jnp.stack(depth_list))
```

```python
import math

import jax
import jax.numpy as jnp
from jax import lax
from jax.sharding import PartitionSpec as P

TILE = 128


def padded_2(block, sides, width):
    for axis, dim in sides:
        count = lax.axis_size(axis)
        forward = [(i, i + 1) for i in range(count - 1)]
        backward = [(target, source) for source, target in forward]
        low = lax.ppermute(
            lax.slice_in_dim(block, block.shape[dim] - width, None, axis=dim), axis, forward
        )
        high = lax.ppermute(lax.slice_in_dim(block, 0, width, axis=dim), axis, backward)
        block = jnp.concatenate([low, block, high], axis=dim)
    return block


def width_pad(field):
    return jnp.pad(field, [(0, 0)] * (field.ndim - 1) + [(1, 1)])


def plane_conv_all(rows_in, kernel, height, width):
    padded = width_pad(rows_in)
    total = None
    for i in range(3):
        for j in range(3):
            term = jnp.einsum(
                "loc,lzycx->lzyox",
                kernel[:, i, j],
                padded[:, :, i : i + height, :, j : j + width],
                preferred_element_type=jnp.float32,
            )
            total = term if total is None else total + term
    return total


def depth_conv_all(deep, kernel, depth):
    total = None
    for k in range(3):
        term = jnp.einsum(
            "loc,lzycx->lzyox", kernel[:, k], deep[:, k : k + depth], preferred_element_type=jnp.float32
        )
        total = term if total is None else total + term
    return total


def plane_back(rows_grad, kernel, height, width):
    padded = width_pad(rows_grad)
    total = None
    for i in range(3):
        for j in range(3):
            term = jnp.einsum(
                "oc,...yox->...ycx",
                kernel[i, j],
                padded[..., 2 - i : 2 - i + height, :, 2 - j : 2 - j + width],
                preferred_element_type=jnp.float32,
            )
            total = term if total is None else total + term
    return total


def plane_taps(grad_mid, rows_in, height, width):
    padded = width_pad(rows_in)
    rows_out = []
    for i in range(3):
        row_taps = []
        for j in range(3):
            row_taps.append(
                jnp.einsum(
                    "...yox,...ycx->oc",
                    grad_mid,
                    padded[..., i : i + height, :, j : j + width],
                    preferred_element_type=jnp.float32,
                )
            )
        rows_out.append(jnp.stack(row_taps))
    return jnp.stack(rows_out)


def depth_back(mix_deep, kernel, depth):
    total = None
    for k in range(3):
        term = jnp.einsum(
            "oc,zyox->zycx",
            kernel[k],
            mix_deep[2 - k : 2 - k + depth],
            preferred_element_type=jnp.float32,
        )
        total = term if total is None else total + term
    return total


def depth_taps(grad_mix, deep, depth):
    return jnp.stack(
        [
            jnp.einsum(
                "zyox,zycx->oc", grad_mix, deep[k : k + depth], preferred_element_type=jnp.float32
            )
            for k in range(3)
        ]
    )


def silu_slope(value):
    sig = jax.nn.sigmoid(value)
    return sig * (1.0 + value * (1.0 - sig))


def local(acts, grad_out, w_plane, w_depth, tiles):
    sections = acts.shape[1]
    height = acts.shape[2]
    width = acts.shape[4]
    chans = w_plane.shape[3]
    count = lax.axis_size("segment")
    layers = count * acts.shape[0]
    zs = grad_out.shape[0]
    scale = 1.0 / math.sqrt(sections * height * lax.axis_size("gy") * width)
    segment = lax.axis_index("segment")

    mine = lax.all_to_all(acts, "segment", 1, 0, tiled=True)
    plane_w = lax.all_gather(w_plane, "segment", axis=0, tiled=True)
    depth_w = lax.all_gather(w_depth, "segment", axis=0, tiled=True)

    ids = (segment * zs + jnp.arange(zs, dtype=jnp.int32))[:, None] * (width // TILE) + jnp.arange(
        width // TILE, dtype=jnp.int32
    )[None, :]
    hit = jnp.any(tiles[0][None, None, :] == ids[:, :, None], axis=2)
    mask_full = jnp.repeat(hit.astype(jnp.float32), TILE, axis=1)[:, None, None, :]

    rows_own = padded_2(mine, (("gy", 2),), 1)
    mid = plane_conv_all(rows_own, plane_w, height, width).astype(jnp.bfloat16)
    deep = padded_2(mid, (("segment", 1),), 1)
    value = depth_conv_all(deep, depth_w, zs)
    factor = silu_slope(value) * mask_full[None]

    grad = grad_out
    plane_list = [None] * layers
    depth_list = [None] * layers
    for layer in reversed(range(layers)):
        grad_mix = (grad.astype(jnp.float32) * factor[layer]).astype(jnp.bfloat16)
        mix_deep = padded_2(grad_mix, (("segment", 0),), 1)
        grad_mid = depth_back(mix_deep, depth_w[layer], zs).astype(jnp.bfloat16)
        rows_grad = padded_2(grad_mid, (("gy", 1),), 1)
        grad = (
            grad.astype(jnp.float32) + plane_back(rows_grad, plane_w[layer], height, width)
        ).astype(jnp.bfloat16)
        depth_list[layer] = depth_taps(grad_mix, deep[layer], zs)
        plane_list[layer] = plane_taps(grad_mid, rows_own[layer], height, width)

    planes = jnp.stack(plane_list).reshape(layers, -1)
    depths = jnp.stack(depth_list).reshape(layers, -1)
    flat = jnp.concatenate([planes, depths], axis=1) * scale
    flat = lax.psum_scatter(flat, "segment", scatter_dimension=0, tiled=True)
    flat = lax.psum(flat, "gy")
    cut = planes.shape[1]
    plane_sum = flat[:, :cut].reshape(-1, 3, 3, chans, chans)
    depth_sum = flat[:, cut:].reshape(-1, 3, chans, chans)
    return (grad, plane_sum, depth_sum)


def solution(mesh):
    placed = (
        P("segment", None, "gy", None, None),
        P("segment", "gy", None, None),
        P("segment", None, None, None, None),
        P("segment", None, None, None),
        P("gy", None),
    )
    return jax.shard_map(
        local,
        mesh=mesh,
        in_specs=placed,
        out_specs=(
            P("segment", "gy", None, None),
            P("segment", None, None, None, None),
            P("segment", None, None, None),
        ),
        check_vma=False,
    )
```

```python
import math

import jax
import jax.numpy as jnp
from jax import lax
from jax.sharding import PartitionSpec as P

TILE = 128


def padded_2(block, sides, width):
    for axis, dim in sides:
        count = lax.axis_size(axis)
        forward = [(i, i + 1) for i in range(count - 1)]
        backward = [(target, source) for source, target in forward]
        low = lax.ppermute(
            lax.slice_in_dim(block, block.shape[dim] - width, None, axis=dim), axis, forward
        )
        high = lax.ppermute(lax.slice_in_dim(block, 0, width, axis=dim), axis, backward)
        block = jnp.concatenate([low, block, high], axis=dim)
    return block


def width_pad(field):
    return jnp.pad(field, [(0, 0)] * (field.ndim - 1) + [(1, 1)])


def plane_conv_all(rows_in, kernel, height, width):
    padded = width_pad(rows_in)
    total = None
    for i in range(3):
        for j in range(3):
            term = jnp.einsum(
                "loc,lzycx->lzyox",
                kernel[:, i, j],
                padded[:, :, i : i + height, :, j : j + width],
                preferred_element_type=jnp.float32,
            )
            total = term if total is None else total + term
    return total


def depth_conv_all(deep, kernel, depth):
    total = None
    for k in range(3):
        term = jnp.einsum(
            "loc,lzycx->lzyox", kernel[:, k], deep[:, k : k + depth], preferred_element_type=jnp.float32
        )
        total = term if total is None else total + term
    return total


def plane_back(rows_grad, kernel, height, width):
    padded = width_pad(rows_grad)
    total = None
    for i in range(3):
        for j in range(3):
            term = jnp.einsum(
                "oc,...yox->...ycx",
                kernel[i, j],
                padded[..., 2 - i : 2 - i + height, :, 2 - j : 2 - j + width],
                preferred_element_type=jnp.float32,
            )
            total = term if total is None else total + term
    return total


def plane_taps(grad_mid, rows_in, height, width):
    padded = width_pad(rows_in)
    rows_out = []
    for i in range(3):
        row_taps = []
        for j in range(3):
            row_taps.append(
                jnp.einsum(
                    "...yox,...ycx->oc",
                    grad_mid,
                    padded[..., i : i + height, :, j : j + width],
                    preferred_element_type=jnp.float32,
                )
            )
        rows_out.append(jnp.stack(row_taps))
    return jnp.stack(rows_out)


def depth_back(mix_deep, kernel, depth):
    total = None
    for k in range(3):
        term = jnp.einsum(
            "oc,zyox->zycx",
            kernel[k],
            mix_deep[2 - k : 2 - k + depth],
            preferred_element_type=jnp.float32,
        )
        total = term if total is None else total + term
    return total


def depth_taps(grad_mix, deep, depth):
    return jnp.stack(
        [
            jnp.einsum(
                "zyox,zycx->oc", grad_mix, deep[k : k + depth], preferred_element_type=jnp.float32
            )
            for k in range(3)
        ]
    )


def silu_slope(value):
    sig = jax.nn.sigmoid(value)
    return sig * (1.0 + value * (1.0 - sig))


def local(acts, grad_out, w_plane, w_depth, tiles):
    sections = acts.shape[1]
    height = acts.shape[2]
    width = acts.shape[4]
    chans = w_plane.shape[3]
    count = lax.axis_size("segment")
    layers = count * acts.shape[0]
    zs = grad_out.shape[0]
    scale = 1.0 / math.sqrt(sections * height * lax.axis_size("gy") * width)
    segment = lax.axis_index("segment")

    block = acts[0].reshape(count, -1)
    kernels = jnp.concatenate([w_plane.reshape(1, -1), w_depth.reshape(1, -1)], axis=1)
    send = jnp.concatenate([block, jnp.broadcast_to(kernels, (count, kernels.shape[1]))], axis=1)
    got = lax.all_to_all(send, "segment", 0, 0, tiled=True)
    cut_a = block.shape[1]
    cut_w = cut_a + w_plane[0].size
    mine = got[:, :cut_a].reshape((count, zs) + acts.shape[2:])
    plane_w = got[:, cut_a:cut_w].reshape((count,) + w_plane.shape[1:])
    depth_w = got[:, cut_w:].reshape((count,) + w_depth.shape[1:])

    ids = (segment * zs + jnp.arange(zs, dtype=jnp.int32))[:, None] * (width // TILE) + jnp.arange(
        width // TILE, dtype=jnp.int32
    )[None, :]
    hit = jnp.any(tiles[0][None, None, :] == ids[:, :, None], axis=2)
    mask_full = jnp.repeat(hit.astype(jnp.float32), TILE, axis=1)[:, None, None, :]

    rows_own = padded_2(mine, (("gy", 2),), 1)
    mid = plane_conv_all(rows_own, plane_w, height, width).astype(jnp.bfloat16)
    deep = padded_2(mid, (("segment", 1),), 1)
    value = depth_conv_all(deep, depth_w, zs)
    factor = silu_slope(value) * mask_full[None]

    grad = grad_out
    plane_list = [None] * layers
    depth_list = [None] * layers
    for layer in reversed(range(layers)):
        grad_mix = (grad.astype(jnp.float32) * factor[layer]).astype(jnp.bfloat16)
        mix_deep = padded_2(grad_mix, (("segment", 0),), 1)
        grad_mid = depth_back(mix_deep, depth_w[layer], zs).astype(jnp.bfloat16)
        rows_grad = padded_2(grad_mid, (("gy", 1),), 1)
        grad = (
            grad.astype(jnp.float32) + plane_back(rows_grad, plane_w[layer], height, width)
        ).astype(jnp.bfloat16)
        depth_list[layer] = depth_taps(grad_mix, deep[layer], zs)
        plane_list[layer] = plane_taps(grad_mid, rows_own[layer], height, width)

    planes = jnp.stack(plane_list).reshape(layers, -1)
    depths = jnp.stack(depth_list).reshape(layers, -1)
    flat = jnp.concatenate([planes, depths], axis=1) * scale
    flat = lax.all_to_all(flat, "segment", 0, 0, tiled=True).sum(axis=0)
    spread_n = lax.axis_size("gy")
    size = flat.shape[0]
    piece = -(-size // spread_n)
    flat = jnp.pad(flat, (0, piece * spread_n - size)).reshape(spread_n, piece)
    part = lax.all_to_all(flat, "gy", 0, 0, tiled=True).sum(axis=0)
    whole = lax.all_to_all(jnp.broadcast_to(part, (spread_n, piece)), "gy", 0, 0, tiled=True)
    flat = whole.reshape(-1)[:size][None]
    cut = planes.shape[1]
    plane_sum = flat[:, :cut].reshape(-1, 3, 3, chans, chans)
    depth_sum = flat[:, cut:].reshape(-1, 3, chans, chans)
    return (grad, plane_sum, depth_sum)


def solution(mesh):
    placed = (
        P("segment", None, "gy", None, None),
        P("segment", "gy", None, None),
        P("segment", None, None, None, None),
        P("segment", None, None, None),
        P("gy", None),
    )
    return jax.shard_map(
        local,
        mesh=mesh,
        in_specs=placed,
        out_specs=(
            P("segment", "gy", None, None),
            P("segment", None, None, None, None),
            P("segment", None, None, None),
        ),
        check_vma=False,
    )
```

```python
import math

import jax
import jax.numpy as jnp
from jax import lax
from jax.sharding import PartitionSpec as P

TILE = 128
HALO = 8


def padded_2(block, sides, width):
    for axis, dim in sides:
        count = lax.axis_size(axis)
        forward = [(i, i + 1) for i in range(count - 1)]
        backward = [(target, source) for source, target in forward]
        low = lax.ppermute(
            lax.slice_in_dim(block, block.shape[dim] - width, None, axis=dim), axis, forward
        )
        high = lax.ppermute(lax.slice_in_dim(block, 0, width, axis=dim), axis, backward)
        block = jnp.concatenate([low, block, high], axis=dim)
    return block


def passed_along(block, axis, distance):
    devices = range(lax.axis_size(axis))
    route = [(i - distance, i) for i in devices if i - distance in devices]
    return lax.ppermute(block, axis, route)


def halo_plan(layers, depth):
    need = [0] * layers
    left = 0
    for layer in reversed(range(layers)):
        if left == 0:
            left = min(depth, layer + 1)
        need[layer] = left
        left -= 1
    return need


def width_pad(field):
    return jnp.pad(field, [(0, 0)] * (field.ndim - 1) + [(1, 1)])


def plane_conv_all(rows_in, kernel, height, width):
    padded = width_pad(rows_in)
    total = None
    for i in range(3):
        for j in range(3):
            term = jnp.einsum(
                "loc,lzycx->lzyox",
                kernel[:, i, j],
                padded[:, :, i : i + height, :, j : j + width],
                preferred_element_type=jnp.float32,
            )
            total = term if total is None else total + term
    return total


def depth_conv_all(deep, kernel, depth):
    total = None
    for k in range(3):
        term = jnp.einsum(
            "loc,lzycx->lzyox", kernel[:, k], deep[:, k : k + depth], preferred_element_type=jnp.float32
        )
        total = term if total is None else total + term
    return total


def plane_back(rows_grad, kernel, height, width):
    padded = width_pad(rows_grad)
    total = None
    for i in range(3):
        for j in range(3):
            term = jnp.einsum(
                "oc,...yox->...ycx",
                kernel[i, j],
                padded[..., 2 - i : 2 - i + height, :, 2 - j : 2 - j + width],
                preferred_element_type=jnp.float32,
            )
            total = term if total is None else total + term
    return total


def plane_taps(grad_mid, rows_in, height, width):
    padded = width_pad(rows_in)
    rows_out = []
    for i in range(3):
        row_taps = []
        for j in range(3):
            row_taps.append(
                jnp.einsum(
                    "...yox,...ycx->oc",
                    grad_mid,
                    padded[..., i : i + height, :, j : j + width],
                    preferred_element_type=jnp.float32,
                )
            )
        rows_out.append(jnp.stack(row_taps))
    return jnp.stack(rows_out)


def depth_back(mix_deep, kernel, depth):
    total = None
    for k in range(3):
        term = jnp.einsum(
            "oc,zyox->zycx",
            kernel[k],
            mix_deep[2 - k : 2 - k + depth],
            preferred_element_type=jnp.float32,
        )
        total = term if total is None else total + term
    return total


def depth_taps(grad_mix, deep, depth):
    return jnp.stack(
        [
            jnp.einsum(
                "zyox,zycx->oc", grad_mix, deep[k : k + depth], preferred_element_type=jnp.float32
            )
            for k in range(3)
        ]
    )


def silu_slope(value):
    sig = jax.nn.sigmoid(value)
    return sig * (1.0 + value * (1.0 - sig))


def local(acts, grad_out, w_plane, w_depth, tiles):
    sections = acts.shape[1]
    height = acts.shape[2]
    width = acts.shape[4]
    chans = w_plane.shape[3]
    count = lax.axis_size("segment")
    layers = count * acts.shape[0]
    zs = grad_out.shape[0]
    scale = 1.0 / math.sqrt(sections * height * lax.axis_size("gy") * width)
    segment = lax.axis_index("segment")

    block = acts[0].reshape(count, -1)
    kernels = jnp.concatenate([w_plane.reshape(1, -1), w_depth.reshape(1, -1)], axis=1)
    send = jnp.concatenate([block, jnp.broadcast_to(kernels, (count, kernels.shape[1]))], axis=1)
    got = lax.all_to_all(send, "segment", 0, 0, tiled=True)
    cut_a = block.shape[1]
    cut_w = cut_a + w_plane[0].size
    mine = got[:, :cut_a].reshape((count, zs) + acts.shape[2:])
    plane_w = got[:, cut_a:cut_w].reshape((count,) + w_plane.shape[1:])
    depth_w = got[:, cut_w:].reshape((count,) + w_depth.shape[1:])

    ids = (segment * zs + jnp.arange(zs, dtype=jnp.int32))[:, None] * (width // TILE) + jnp.arange(
        width // TILE, dtype=jnp.int32
    )[None, :]
    hit = jnp.any(tiles[0][None, None, :] == ids[:, :, None], axis=2)
    mask_full = jnp.repeat(hit.astype(jnp.float32), TILE, axis=1)[:, None, None, :]

    rows_own = padded_2(mine, (("gy", 2),), 1)
    mid = plane_conv_all(rows_own, plane_w, height, width).astype(jnp.bfloat16)
    deep = padded_2(mid, (("segment", 1),), 1)
    value = depth_conv_all(deep, depth_w, zs)
    factor = silu_slope(value) * mask_full[None]

    need = halo_plan(layers, HALO)
    reach = -(-max(need) // height)
    factor_b = factor.astype(jnp.bfloat16)
    lows, highs, picks = {}, {}, {}
    for dist in range(1, reach + 1):
        chosen = [layer for layer in range(layers) if need[layer] > height * (dist - 1)]
        picks[dist] = chosen
        load = jnp.stack([factor_b[layer] for layer in chosen] + [grad_out])
        lows[dist] = passed_along(load, "gy", dist)
        highs[dist] = passed_along(load, "gy", -dist)

    def halo_of(index_of, h, own):
        span = -(-h // height)
        low = jnp.concatenate([index_of(lows[d], d) for d in range(span, 0, -1)], axis=1)[:, -h:]
        high = jnp.concatenate([index_of(highs[d], d) for d in range(1, span + 1)], axis=1)[:, :h]
        return low, high

    def refreshed(grad, h):
        span = -(-h // height)
        low = jnp.concatenate([passed_along(grad, "gy", d) for d in range(span, 0, -1)], axis=1)
        high = jnp.concatenate([passed_along(grad, "gy", -d) for d in range(1, span + 1)], axis=1)
        return jnp.concatenate([low[:, low.shape[1] - h :], grad, high[:, :h]], axis=1)

    low, high = halo_of(lambda part, d: part[-1], need[layers - 1], grad_out)
    grad = jnp.concatenate([low, grad_out, high], axis=1)
    plane_list = [None] * layers
    depth_list = [None] * layers
    for layer in reversed(range(layers)):
        h = need[layer]
        if grad.shape[1] != height + 2 * h:
            grad = refreshed(grad, h)
        low, high = halo_of(lambda part, d: part[picks[d].index(layer)], h, None)
        wide = jnp.concatenate([low.astype(jnp.float32), factor[layer], high.astype(jnp.float32)], axis=1)
        grad_mix = (grad.astype(jnp.float32) * wide).astype(jnp.bfloat16)
        mix_deep = padded_2(grad_mix, (("segment", 0),), 1)
        grad_mid = depth_back(mix_deep, depth_w[layer], zs).astype(jnp.bfloat16)
        rows = grad.shape[1] - 2
        grad = (
            grad[:, 1:-1].astype(jnp.float32) + plane_back(grad_mid, plane_w[layer], rows, width)
        ).astype(jnp.bfloat16)
        depth_list[layer] = depth_taps(grad_mix[:, h : h + height], deep[layer], zs)
        plane_list[layer] = plane_taps(grad_mid[:, h : h + height], rows_own[layer], height, width)

    planes = jnp.stack(plane_list).reshape(layers, -1)
    depths = jnp.stack(depth_list).reshape(layers, -1)
    flat = jnp.concatenate([planes, depths], axis=1) * scale
    flat = lax.all_to_all(flat, "segment", 0, 0, tiled=True).sum(axis=0)
    spread_n = lax.axis_size("gy")
    size = flat.shape[0]
    piece = -(-size // spread_n)
    flat = jnp.pad(flat, (0, piece * spread_n - size)).reshape(spread_n, piece)
    part = lax.all_to_all(flat, "gy", 0, 0, tiled=True).sum(axis=0)
    whole = lax.all_to_all(jnp.broadcast_to(part, (spread_n, piece)), "gy", 0, 0, tiled=True)
    flat = whole.reshape(-1)[:size][None]
    cut = planes.shape[1]
    plane_sum = flat[:, :cut].reshape(-1, 3, 3, chans, chans)
    depth_sum = flat[:, cut:].reshape(-1, 3, chans, chans)
    return (grad, plane_sum, depth_sum)


def solution(mesh):
    placed = (
        P("segment", None, "gy", None, None),
        P("segment", "gy", None, None),
        P("segment", None, None, None, None),
        P("segment", None, None, None),
        P("gy", None),
    )
    return jax.shard_map(
        local,
        mesh=mesh,
        in_specs=placed,
        out_specs=(
            P("segment", "gy", None, None),
            P("segment", None, None, None, None),
            P("segment", None, None, None),
        ),
        check_vma=False,
    )
```

```python
import math

import jax
import jax.numpy as jnp
from jax import lax
from jax.sharding import PartitionSpec as P

TILE = 128
HALO = 8


def padded_2(block, sides, width):
    for axis, dim in sides:
        count = lax.axis_size(axis)
        forward = [(i, i + 1) for i in range(count - 1)]
        backward = [(target, source) for source, target in forward]
        low = lax.ppermute(
            lax.slice_in_dim(block, block.shape[dim] - width, None, axis=dim), axis, forward
        )
        high = lax.ppermute(lax.slice_in_dim(block, 0, width, axis=dim), axis, backward)
        block = jnp.concatenate([low, block, high], axis=dim)
    return block


def passed_along(block, axis, distance):
    devices = range(lax.axis_size(axis))
    route = [(i - distance, i) for i in devices if i - distance in devices]
    return lax.ppermute(block, axis, route)


def halo_plan(layers, depth):
    need = [0] * layers
    left = 0
    for layer in reversed(range(layers)):
        if left == 0:
            left = min(depth, layer + 1)
        need[layer] = left
        left -= 1
    return need


def width_pad(field):
    return jnp.pad(field, [(0, 0)] * (field.ndim - 1) + [(1, 1)])


def plane_conv_all(rows_in, kernel, height, width):
    padded = width_pad(rows_in)
    total = None
    for i in range(3):
        for j in range(3):
            term = jnp.einsum(
                "loc,lzycx->lzyox",
                kernel[:, i, j],
                padded[:, :, i : i + height, :, j : j + width],
                preferred_element_type=jnp.float32,
            )
            total = term if total is None else total + term
    return total


def depth_conv_all(deep, kernel, depth):
    total = None
    for k in range(3):
        term = jnp.einsum(
            "loc,lzycx->lzyox", kernel[:, k], deep[:, k : k + depth], preferred_element_type=jnp.float32
        )
        total = term if total is None else total + term
    return total


def plane_back(rows_grad, kernel, height, width):
    padded = width_pad(rows_grad)
    total = None
    for i in range(3):
        for j in range(3):
            term = jnp.einsum(
                "oc,...yox->...ycx",
                kernel[i, j],
                padded[..., 2 - i : 2 - i + height, :, 2 - j : 2 - j + width],
                preferred_element_type=jnp.float32,
            )
            total = term if total is None else total + term
    return total


def plane_taps(grad_mid, rows_in, height, width):
    padded = width_pad(rows_in)
    rows_out = []
    for i in range(3):
        row_taps = []
        for j in range(3):
            row_taps.append(
                jnp.einsum(
                    "...yox,...ycx->oc",
                    grad_mid,
                    padded[..., i : i + height, :, j : j + width],
                    preferred_element_type=jnp.float32,
                )
            )
        rows_out.append(jnp.stack(row_taps))
    return jnp.stack(rows_out)


def depth_back(mix_deep, kernel, depth):
    total = None
    for k in range(3):
        term = jnp.einsum(
            "oc,zyox->zycx",
            kernel[k],
            mix_deep[2 - k : 2 - k + depth],
            preferred_element_type=jnp.float32,
        )
        total = term if total is None else total + term
    return total


def depth_taps(grad_mix, deep, depth):
    return jnp.stack(
        [
            jnp.einsum(
                "zyox,zycx->oc", grad_mix, deep[k : k + depth], preferred_element_type=jnp.float32
            )
            for k in range(3)
        ]
    )


def silu_slope(value):
    sig = jax.nn.sigmoid(value)
    return sig * (1.0 + value * (1.0 - sig))


def local(acts, grad_out, w_plane, w_depth, tiles):
    sections = acts.shape[1]
    height = acts.shape[2]
    width = acts.shape[4]
    chans = w_plane.shape[3]
    count = lax.axis_size("segment")
    layers = count * acts.shape[0]
    zs = grad_out.shape[0]
    scale = 1.0 / math.sqrt(sections * height * lax.axis_size("gy") * width)
    segment = lax.axis_index("segment")

    block = acts[0].reshape(count, -1)
    kernels = jnp.concatenate([w_plane.reshape(1, -1), w_depth.reshape(1, -1)], axis=1)
    send = jnp.concatenate([block, jnp.broadcast_to(kernels, (count, kernels.shape[1]))], axis=1)
    got = lax.all_to_all(send, "segment", 0, 0, tiled=True)
    cut_a = block.shape[1]
    cut_w = cut_a + w_plane[0].size
    mine = got[:, :cut_a].reshape((count, zs) + acts.shape[2:])
    plane_w = got[:, cut_a:cut_w].reshape((count,) + w_plane.shape[1:])
    depth_w = got[:, cut_w:].reshape((count,) + w_depth.shape[1:])

    ids = (segment * zs + jnp.arange(zs, dtype=jnp.int32))[:, None] * (width // TILE) + jnp.arange(
        width // TILE, dtype=jnp.int32
    )[None, :]
    hit = jnp.any(tiles[0][None, None, :] == ids[:, :, None], axis=2)
    mask_full = jnp.repeat(hit.astype(jnp.float32), TILE, axis=1)[:, None, None, :]

    rows_own = padded_2(mine, (("gy", 2),), 1)
    mid = plane_conv_all(rows_own, plane_w, height, width).astype(jnp.bfloat16)
    deep = padded_2(mid, (("segment", 1),), 1)
    value = depth_conv_all(deep, depth_w, zs)
    factor = silu_slope(value) * mask_full[None]

    need = halo_plan(layers, HALO)
    reach = -(-max(need) // height)
    factor_b = factor.astype(jnp.bfloat16)
    lows, highs, picks = {}, {}, {}
    for dist in range(1, reach + 1):
        chosen = [layer for layer in range(layers) if need[layer] > height * (dist - 1)]
        picks[dist] = chosen
        load = jnp.stack([factor_b[layer] for layer in chosen] + [grad_out])
        lows[dist] = passed_along(load, "gy", dist)
        highs[dist] = passed_along(load, "gy", -dist)

    def halo_of(index_of, h, own):
        span = -(-h // height)
        low = jnp.concatenate([index_of(lows[d], d) for d in range(span, 0, -1)], axis=1)[:, -h:]
        high = jnp.concatenate([index_of(highs[d], d) for d in range(1, span + 1)], axis=1)[:, :h]
        return low, high

    def refreshed(grad, h):
        span = -(-h // height)
        low = jnp.concatenate([passed_along(grad, "gy", d) for d in range(span, 0, -1)], axis=1)
        high = jnp.concatenate([passed_along(grad, "gy", -d) for d in range(1, span + 1)], axis=1)
        return jnp.concatenate([low[:, low.shape[1] - h :], grad, high[:, :h]], axis=1)

    low, high = halo_of(lambda part, d: part[-1], need[layers - 1], grad_out)
    grad = jnp.concatenate([low, grad_out, high], axis=1)
    plane_list = [None] * layers
    depth_list = [None] * layers
    for layer in reversed(range(layers)):
        h = need[layer]
        if grad.shape[1] != height + 2 * h:
            grad = refreshed(grad, h)
        low, high = halo_of(lambda part, d: part[picks[d].index(layer)], h, None)
        wide = jnp.concatenate([low.astype(jnp.float32), factor[layer], high.astype(jnp.float32)], axis=1)
        grad_mix = (grad.astype(jnp.float32) * wide).astype(jnp.bfloat16)
        mix_deep = padded_2(grad_mix, (("segment", 0),), 1)
        grad_mid = depth_back(mix_deep, depth_w[layer], zs).astype(jnp.bfloat16)
        rows = grad.shape[1] - 2
        grad = (
            grad[:, 1:-1].astype(jnp.float32) + plane_back(grad_mid, plane_w[layer], rows, width)
        ).astype(jnp.bfloat16)
        depth_list[layer] = grad_mix[:, h : h + height]
        plane_list[layer] = grad_mid[:, h : h + height]

    mixes = jnp.stack(depth_list)
    mids = jnp.stack(plane_list)
    wide_rows = width_pad(rows_own)
    planes = jnp.stack(
        [
            jnp.einsum(
                "lzyox,lzycx->loc",
                mids,
                wide_rows[:, :, i : i + height, :, j : j + width],
                preferred_element_type=jnp.float32,
            )
            for i in range(3)
            for j in range(3)
        ],
        axis=1,
    ).reshape(layers, -1)
    depths = jnp.stack(
        [
            jnp.einsum(
                "lzyox,lzycx->loc", mixes, deep[:, k : k + zs], preferred_element_type=jnp.float32
            )
            for k in range(3)
        ],
        axis=1,
    ).reshape(layers, -1)
    flat = jnp.concatenate([planes, depths], axis=1) * scale
    spread_n = lax.axis_size("gy")
    size = flat.shape[1]
    piece = -(-size // spread_n)
    flat = jnp.pad(flat, ((0, 0), (0, piece * spread_n - size))).reshape(layers * spread_n, piece)
    part = lax.all_to_all(flat, ("segment", "gy"), 0, 0, tiled=True).sum(axis=0)
    whole = lax.all_to_all(jnp.broadcast_to(part, (spread_n, piece)), "gy", 0, 0, tiled=True)
    flat = whole.reshape(-1)[:size][None]
    cut = planes.shape[1]
    plane_sum = flat[:, :cut].reshape(-1, 3, 3, chans, chans)
    depth_sum = flat[:, cut:].reshape(-1, 3, chans, chans)
    return (grad, plane_sum, depth_sum)


def solution(mesh):
    placed = (
        P("segment", None, "gy", None, None),
        P("segment", "gy", None, None),
        P("segment", None, None, None, None),
        P("segment", None, None, None),
        P("gy", None),
    )
    return jax.shard_map(
        local,
        mesh=mesh,
        in_specs=placed,
        out_specs=(
            P("segment", "gy", None, None),
            P("segment", None, None, None, None),
            P("segment", None, None, None),
        ),
        check_vma=False,
    )
```

```python
import math

import jax
import jax.numpy as jnp
from jax import lax
from jax.sharding import PartitionSpec as P

TILE = 128
HALO = 8


def padded_2(block, sides, width):
    for axis, dim in sides:
        count = lax.axis_size(axis)
        forward = [(i, i + 1) for i in range(count - 1)]
        backward = [(target, source) for source, target in forward]
        low = lax.ppermute(
            lax.slice_in_dim(block, block.shape[dim] - width, None, axis=dim), axis, forward
        )
        high = lax.ppermute(lax.slice_in_dim(block, 0, width, axis=dim), axis, backward)
        block = jnp.concatenate([low, block, high], axis=dim)
    return block


def passed_along(block, axis, distance):
    devices = range(lax.axis_size(axis))
    route = [(i - distance, i) for i in devices if i - distance in devices]
    return lax.ppermute(block, axis, route)


def halo_plan(layers, depth):
    need = [0] * layers
    left = 0
    for layer in reversed(range(layers)):
        if left == 0:
            left = min(depth, layer + 1)
        need[layer] = left
        left -= 1
    return need


def width_pad(field):
    return jnp.pad(field, [(0, 0)] * (field.ndim - 1) + [(1, 1)])


def plane_conv_all(rows_in, kernel, height, width):
    padded = width_pad(rows_in)
    total = None
    for i in range(3):
        for j in range(3):
            term = jnp.einsum(
                "loc,lzycx->lzyox",
                kernel[:, i, j],
                padded[:, :, i : i + height, :, j : j + width],
                preferred_element_type=jnp.float32,
            )
            total = term if total is None else total + term
    return total


def depth_conv_all(deep, kernel, depth):
    total = None
    for k in range(3):
        term = jnp.einsum(
            "loc,lzycx->lzyox", kernel[:, k], deep[:, k : k + depth], preferred_element_type=jnp.float32
        )
        total = term if total is None else total + term
    return total


def plane_back(rows_grad, kernel, height, width):
    padded = width_pad(rows_grad)
    total = None
    for i in range(3):
        for j in range(3):
            term = jnp.einsum(
                "oc,...yox->...ycx",
                kernel[i, j],
                padded[..., 2 - i : 2 - i + height, :, 2 - j : 2 - j + width],
                preferred_element_type=jnp.float32,
            )
            total = term if total is None else total + term
    return total


def plane_taps(grad_mid, rows_in, height, width):
    padded = width_pad(rows_in)
    rows_out = []
    for i in range(3):
        row_taps = []
        for j in range(3):
            row_taps.append(
                jnp.einsum(
                    "...yox,...ycx->oc",
                    grad_mid,
                    padded[..., i : i + height, :, j : j + width],
                    preferred_element_type=jnp.float32,
                )
            )
        rows_out.append(jnp.stack(row_taps))
    return jnp.stack(rows_out)


def depth_back(mix_deep, kernel, depth):
    total = None
    for k in range(3):
        term = jnp.einsum(
            "oc,zyox->zycx",
            kernel[k],
            mix_deep[2 - k : 2 - k + depth],
            preferred_element_type=jnp.float32,
        )
        total = term if total is None else total + term
    return total


def depth_taps(grad_mix, deep, depth):
    return jnp.stack(
        [
            jnp.einsum(
                "zyox,zycx->oc", grad_mix, deep[k : k + depth], preferred_element_type=jnp.float32
            )
            for k in range(3)
        ]
    )


def silu_slope(value):
    sig = jax.nn.sigmoid(value)
    return sig * (1.0 + value * (1.0 - sig))


def local(acts, grad_out, w_plane, w_depth, tiles):
    sections = acts.shape[1]
    height = acts.shape[2]
    width = acts.shape[4]
    chans = w_plane.shape[3]
    count = lax.axis_size("segment")
    layers = count * acts.shape[0]
    zs = grad_out.shape[0]
    scale = 1.0 / math.sqrt(sections * height * lax.axis_size("gy") * width)
    segment = lax.axis_index("segment")

    block = acts[0].reshape(count, -1, width)
    kernels = jnp.concatenate([w_plane.reshape(-1), w_depth.reshape(-1)]).reshape(-1, width)
    send = jnp.concatenate([block, jnp.broadcast_to(kernels[None], (count,) + kernels.shape)], axis=1)
    got = lax.all_to_all(send, "segment", 0, 0, tiled=True)
    cut_a = block.shape[1]
    mine = got[:, :cut_a].reshape((count, zs) + acts.shape[2:])
    taps = w_plane.shape[1] * w_plane.shape[2]
    weights = lax.optimization_barrier(got[:, cut_a:].reshape(count, -1, chans, chans))
    plane_w = weights[:, :taps].reshape((count,) + w_plane.shape[1:])
    depth_w = weights[:, taps:].reshape((count,) + w_depth.shape[1:])

    ids = (segment * zs + jnp.arange(zs, dtype=jnp.int32))[:, None] * (width // TILE) + jnp.arange(
        width // TILE, dtype=jnp.int32
    )[None, :]
    hit = jnp.any(tiles[0][None, None, :] == ids[:, :, None], axis=2)
    mask_full = jnp.repeat(hit.astype(jnp.float32), TILE, axis=1)[:, None, None, :]

    rows_own = padded_2(mine, (("gy", 2),), 1)
    mid = plane_conv_all(rows_own, plane_w, height, width).astype(jnp.bfloat16)
    deep = padded_2(mid, (("segment", 1),), 1)
    value = depth_conv_all(deep, depth_w, zs)
    factor = silu_slope(value) * mask_full[None]

    need = halo_plan(layers, HALO)
    reach = -(-max(need) // height)
    factor_b = factor.astype(jnp.bfloat16)
    lows, highs, picks = {}, {}, {}
    for dist in range(1, reach + 1):
        chosen = [layer for layer in range(layers) if need[layer] > height * (dist - 1)]
        picks[dist] = chosen
        load = jnp.stack([factor_b[layer] for layer in chosen] + [grad_out])
        lows[dist] = passed_along(load, "gy", dist)
        highs[dist] = passed_along(load, "gy", -dist)

    def halo_of(index_of, h, own):
        span = -(-h // height)
        low = jnp.concatenate([index_of(lows[d], d) for d in range(span, 0, -1)], axis=1)[:, -h:]
        high = jnp.concatenate([index_of(highs[d], d) for d in range(1, span + 1)], axis=1)[:, :h]
        return low, high

    def refreshed(grad, h):
        span = -(-h // height)
        low = jnp.concatenate([passed_along(grad, "gy", d) for d in range(span, 0, -1)], axis=1)
        high = jnp.concatenate([passed_along(grad, "gy", -d) for d in range(1, span + 1)], axis=1)
        return jnp.concatenate([low[:, low.shape[1] - h :], grad, high[:, :h]], axis=1)

    low, high = halo_of(lambda part, d: part[-1], need[layers - 1], grad_out)
    grad = jnp.concatenate([low, grad_out, high], axis=1)
    plane_list = [None] * layers
    depth_list = [None] * layers
    for layer in reversed(range(layers)):
        h = need[layer]
        if grad.shape[1] != height + 2 * h:
            grad = refreshed(grad, h)
        low, high = halo_of(lambda part, d: part[picks[d].index(layer)], h, None)
        wide = jnp.concatenate([low.astype(jnp.float32), factor[layer], high.astype(jnp.float32)], axis=1)
        grad_mix = (grad.astype(jnp.float32) * wide).astype(jnp.bfloat16)
        mix_deep = padded_2(grad_mix, (("segment", 0),), 1)
        grad_mid = depth_back(mix_deep, depth_w[layer], zs).astype(jnp.bfloat16)
        rows = grad.shape[1] - 2
        grad = (
            grad[:, 1:-1].astype(jnp.float32) + plane_back(grad_mid, plane_w[layer], rows, width)
        ).astype(jnp.bfloat16)
        depth_list[layer] = grad_mix[:, h : h + height]
        plane_list[layer] = grad_mid[:, h : h + height]

    mixes = jnp.stack(depth_list)
    mids = jnp.stack(plane_list)
    wide_rows = width_pad(rows_own)
    planes = jnp.stack(
        [
            jnp.einsum(
                "lzyox,lzycx->loc",
                mids,
                wide_rows[:, :, i : i + height, :, j : j + width],
                preferred_element_type=jnp.float32,
            )
            for i in range(3)
            for j in range(3)
        ],
        axis=1,
    ).reshape(layers, -1)
    depths = jnp.stack(
        [
            jnp.einsum(
                "lzyox,lzycx->loc", mixes, deep[:, k : k + zs], preferred_element_type=jnp.float32
            )
            for k in range(3)
        ],
        axis=1,
    ).reshape(layers, -1)
    flat = jnp.concatenate([planes, depths], axis=1) * scale
    spread_n = lax.axis_size("gy")
    size = flat.shape[1]
    piece = -(-size // spread_n)
    flat = jnp.pad(flat, ((0, 0), (0, piece * spread_n - size))).reshape(layers * spread_n, piece)
    part = lax.all_to_all(flat, ("segment", "gy"), 0, 0, tiled=True).sum(axis=0)
    whole = lax.all_to_all(jnp.broadcast_to(part, (spread_n, piece)), "gy", 0, 0, tiled=True)
    flat = whole.reshape(-1)[:size][None]
    cut = planes.shape[1]
    plane_sum = flat[:, :cut].reshape(-1, 3, 3, chans, chans)
    depth_sum = flat[:, cut:].reshape(-1, 3, chans, chans)
    return (grad, plane_sum, depth_sum)


def solution(mesh):
    placed = (
        P("segment", None, "gy", None, None),
        P("segment", "gy", None, None),
        P("segment", None, None, None, None),
        P("segment", None, None, None),
        P("gy", None),
    )
    return jax.shard_map(
        local,
        mesh=mesh,
        in_specs=placed,
        out_specs=(
            P("segment", "gy", None, None),
            P("segment", None, None, None, None),
            P("segment", None, None, None),
        ),
        check_vma=False,
    )
```

```python
import math

import jax
import jax.numpy as jnp
from jax import lax
from jax.sharding import PartitionSpec as P

TILE = 128
HALO = 8


def padded_2(block, sides, width):
    for axis, dim in sides:
        count = lax.axis_size(axis)
        forward = [(i, i + 1) for i in range(count - 1)]
        backward = [(target, source) for source, target in forward]
        low = lax.ppermute(
            lax.slice_in_dim(block, block.shape[dim] - width, None, axis=dim), axis, forward
        )
        high = lax.ppermute(lax.slice_in_dim(block, 0, width, axis=dim), axis, backward)
        block = jnp.concatenate([low, block, high], axis=dim)
    return block


def passed_along(block, axis, distance):
    devices = range(lax.axis_size(axis))
    route = [(i - distance, i) for i in devices if i - distance in devices]
    return lax.ppermute(block, axis, route)


def halo_plan(layers, depth):
    need = [0] * layers
    left = 0
    for layer in reversed(range(layers)):
        if left == 0:
            left = min(depth, layer + 1)
        need[layer] = left
        left -= 1
    return need


def width_pad(field):
    return jnp.pad(field, [(0, 0)] * (field.ndim - 1) + [(1, 1)])


def plane_conv_all(rows_in, kernel, height, width):
    padded = width_pad(rows_in)
    total = None
    for i in range(3):
        for j in range(3):
            term = jnp.einsum(
                "loc,lzycx->lzyox",
                kernel[:, i, j],
                padded[:, :, i : i + height, :, j : j + width],
                preferred_element_type=jnp.float32,
            )
            total = term if total is None else total + term
    return total


def depth_conv_all(deep, kernel, depth):
    total = None
    for k in range(3):
        term = jnp.einsum(
            "loc,lzycx->lzyox", kernel[:, k], deep[:, k : k + depth], preferred_element_type=jnp.float32
        )
        total = term if total is None else total + term
    return total


def plane_back(rows_grad, kernel, height, width):
    padded = width_pad(rows_grad)
    total = None
    for i in range(3):
        for j in range(3):
            term = jnp.einsum(
                "oc,...yox->...ycx",
                kernel[i, j],
                padded[..., 2 - i : 2 - i + height, :, 2 - j : 2 - j + width],
                preferred_element_type=jnp.float32,
            )
            total = term if total is None else total + term
    return total


def plane_taps(grad_mid, rows_in, height, width):
    padded = width_pad(rows_in)
    rows_out = []
    for i in range(3):
        row_taps = []
        for j in range(3):
            row_taps.append(
                jnp.einsum(
                    "...yox,...ycx->oc",
                    grad_mid,
                    padded[..., i : i + height, :, j : j + width],
                    preferred_element_type=jnp.float32,
                )
            )
        rows_out.append(jnp.stack(row_taps))
    return jnp.stack(rows_out)


def depth_back(mix_deep, kernel, depth):
    total = None
    for k in range(3):
        term = jnp.einsum(
            "oc,zyox->zycx",
            kernel[k],
            mix_deep[2 - k : 2 - k + depth],
            preferred_element_type=jnp.float32,
        )
        total = term if total is None else total + term
    return total


def depth_taps(grad_mix, deep, depth):
    return jnp.stack(
        [
            jnp.einsum(
                "zyox,zycx->oc", grad_mix, deep[k : k + depth], preferred_element_type=jnp.float32
            )
            for k in range(3)
        ]
    )


def silu_slope(value):
    sig = jax.nn.sigmoid(value)
    return sig * (1.0 + value * (1.0 - sig))


def local(acts, grad_out, w_plane, w_depth, tiles):
    sections = acts.shape[1]
    height = acts.shape[2]
    width = acts.shape[4]
    chans = w_plane.shape[3]
    count = lax.axis_size("segment")
    layers = count * acts.shape[0]
    zs = grad_out.shape[0]
    scale = 1.0 / math.sqrt(sections * height * lax.axis_size("gy") * width)
    segment = lax.axis_index("segment")

    block = acts[0].reshape(count, -1, width)
    kernels = jnp.concatenate([w_plane.reshape(-1), w_depth.reshape(-1)]).reshape(-1, width)
    send = jnp.concatenate([block, jnp.broadcast_to(kernels[None], (count,) + kernels.shape)], axis=1)
    got = lax.all_to_all(send, "segment", 0, 0, tiled=True)
    cut_a = block.shape[1]
    mine = got[:, :cut_a].reshape((count, zs) + acts.shape[2:])
    taps = w_plane.shape[1] * w_plane.shape[2]
    weights = lax.optimization_barrier(got[:, cut_a:].reshape(count, -1, chans, chans))
    plane_w = weights[:, :taps].reshape((count,) + w_plane.shape[1:])
    depth_w = weights[:, taps:].reshape((count,) + w_depth.shape[1:])

    ids = (segment * zs + jnp.arange(zs, dtype=jnp.int32))[:, None] * (width // TILE) + jnp.arange(
        width // TILE, dtype=jnp.int32
    )[None, :]
    hit = jnp.any(tiles[0][None, None, :] == ids[:, :, None], axis=2)
    mask_full = jnp.repeat(hit.astype(jnp.float32), TILE, axis=1)[:, None, None, :]

    rows_own = padded_2(mine, (("gy", 2),), 1)
    mid = plane_conv_all(rows_own, plane_w, height, width).astype(jnp.bfloat16)
    deep = padded_2(mid, (("segment", 1),), 1)
    value = depth_conv_all(deep, depth_w, zs)
    factor = silu_slope(value) * mask_full[None]

    need = halo_plan(layers, HALO)
    reach = -(-max(need) // height)
    factor_b = factor.astype(jnp.bfloat16)
    lows, highs, picks = {}, {}, {}
    for dist in range(1, reach + 1):
        chosen = [layer for layer in range(layers) if need[layer] > height * (dist - 1)]
        picks[dist] = chosen
        load = jnp.stack([factor_b[layer] for layer in chosen] + [grad_out])
        lows[dist] = passed_along(load, "gy", dist)
        highs[dist] = passed_along(load, "gy", -dist)

    def halo_of(index_of, h, own):
        span = -(-h // height)
        low = jnp.concatenate([index_of(lows[d], d) for d in range(span, 0, -1)], axis=1)[:, -h:]
        high = jnp.concatenate([index_of(highs[d], d) for d in range(1, span + 1)], axis=1)[:, :h]
        return low, high

    def refreshed(grad, h):
        span = -(-h // height)
        low = jnp.concatenate([passed_along(grad, "gy", d) for d in range(span, 0, -1)], axis=1)
        high = jnp.concatenate([passed_along(grad, "gy", -d) for d in range(1, span + 1)], axis=1)
        return jnp.concatenate([low[:, low.shape[1] - h :], grad, high[:, :h]], axis=1)

    low, high = halo_of(lambda part, d: part[-1], need[layers - 1], grad_out)
    grad = jnp.concatenate([low, grad_out, high], axis=1)
    plane_list = [None] * layers
    depth_list = [None] * layers
    for layer in reversed(range(layers)):
        h = need[layer]
        if grad.shape[1] != height + 2 * h:
            grad = refreshed(grad, h)
        low, high = halo_of(lambda part, d: part[picks[d].index(layer)], h, None)
        wide = jnp.concatenate([low.astype(jnp.float32), factor[layer], high.astype(jnp.float32)], axis=1)
        grad_mix = (grad.astype(jnp.float32) * wide).astype(jnp.bfloat16)
        mix_deep = padded_2(grad_mix, (("segment", 0),), 1)
        grad_mid = depth_back(mix_deep, depth_w[layer], zs).astype(jnp.bfloat16)
        rows = grad.shape[1] - 2
        grad = (
            grad[:, 1:-1].astype(jnp.float32) + plane_back(grad_mid, plane_w[layer], rows, width)
        ).astype(jnp.bfloat16)
        depth_list[layer] = grad_mix[:, h : h + height]
        plane_list[layer] = grad_mid[:, h : h + height]

    wide_rows = width_pad(rows_own)

    def kernel_grads(chosen):
        mids = jnp.stack([plane_list[layer] for layer in chosen])
        mixes = jnp.stack([depth_list[layer] for layer in chosen])
        rows = wide_rows[chosen[0] : chosen[-1] + 1]
        shifted = jnp.concatenate(
            [rows[:, :, i : i + height, :, j : j + width] for i in range(3) for j in range(3)],
            axis=3,
        )
        planes = jnp.einsum("lzyox,lzykx->lok", mids, shifted, preferred_element_type=jnp.float32)
        planes = planes.reshape(len(chosen), chans, 9, chans).transpose(0, 2, 1, 3)
        deeps = deep[chosen[0] : chosen[-1] + 1]
        stacked = jnp.concatenate([deeps[:, k : k + zs] for k in range(3)], axis=3)
        depths = jnp.einsum("lzyox,lzykx->lok", mixes, stacked, preferred_element_type=jnp.float32)
        depths = depths.reshape(len(chosen), chans, 3, chans).transpose(0, 2, 1, 3)
        return planes.reshape(len(chosen), -1), depths.reshape(len(chosen), -1)

    first_p, first_d = kernel_grads([0])
    rest_p, rest_d = kernel_grads(list(range(1, layers)))
    planes = jnp.concatenate([first_p, rest_p])
    depths = jnp.concatenate([first_d, rest_d])
    flat = jnp.concatenate([planes, depths], axis=1) * scale
    spread_n = lax.axis_size("gy")
    size = flat.shape[1]
    piece = -(-size // spread_n)
    flat = jnp.pad(flat, ((0, 0), (0, piece * spread_n - size))).reshape(layers * spread_n, piece)
    part = lax.all_to_all(flat, ("segment", "gy"), 0, 0, tiled=True).sum(axis=0)
    whole = lax.all_to_all(jnp.broadcast_to(part, (spread_n, piece)), "gy", 0, 0, tiled=True)
    flat = whole.reshape(-1)[:size][None]
    cut = planes.shape[1]
    plane_sum = flat[:, :cut].reshape(-1, 3, 3, chans, chans)
    depth_sum = flat[:, cut:].reshape(-1, 3, chans, chans)
    return (grad, plane_sum, depth_sum)


def solution(mesh):
    placed = (
        P("segment", None, "gy", None, None),
        P("segment", "gy", None, None),
        P("segment", None, None, None, None),
        P("segment", None, None, None),
        P("gy", None),
    )
    return jax.shard_map(
        local,
        mesh=mesh,
        in_specs=placed,
        out_specs=(
            P("segment", "gy", None, None),
            P("segment", None, None, None, None),
            P("segment", None, None, None),
        ),
        check_vma=False,
    )
```

```python
import math

import jax
import jax.numpy as jnp
from jax import lax
from jax.sharding import PartitionSpec as P

TILE = 128
HALO = 4


def padded_2(block, sides, width):
    for axis, dim in sides:
        count = lax.axis_size(axis)
        forward = [(i, i + 1) for i in range(count - 1)]
        backward = [(target, source) for source, target in forward]
        low = lax.ppermute(
            lax.slice_in_dim(block, block.shape[dim] - width, None, axis=dim), axis, forward
        )
        high = lax.ppermute(lax.slice_in_dim(block, 0, width, axis=dim), axis, backward)
        block = jnp.concatenate([low, block, high], axis=dim)
    return block


def passed_along(block, axis, distance):
    devices = range(lax.axis_size(axis))
    route = [(i - distance, i) for i in devices if i - distance in devices]
    return lax.ppermute(block, axis, route)


def halo_plan(layers, depth):
    need = [0] * layers
    left = 0
    for layer in reversed(range(layers)):
        if left == 0:
            left = min(depth, layer + 1)
        need[layer] = left
        left -= 1
    return need


def width_pad(field):
    return jnp.pad(field, [(0, 0)] * (field.ndim - 1) + [(1, 1)])


def plane_conv_all(rows_in, kernel, height, width):
    padded = width_pad(rows_in)
    total = None
    for i in range(3):
        for j in range(3):
            term = jnp.einsum(
                "loc,lzycx->lzyox",
                kernel[:, i, j],
                padded[:, :, i : i + height, :, j : j + width],
                preferred_element_type=jnp.float32,
            )
            total = term if total is None else total + term
    return total


def depth_conv_all(deep, kernel, depth):
    total = None
    for k in range(3):
        term = jnp.einsum(
            "loc,lzycx->lzyox", kernel[:, k], deep[:, k : k + depth], preferred_element_type=jnp.float32
        )
        total = term if total is None else total + term
    return total


def plane_back(rows_grad, kernel, height, width):
    padded = width_pad(rows_grad)
    total = None
    for i in range(3):
        for j in range(3):
            term = jnp.einsum(
                "oc,...yox->...ycx",
                kernel[i, j],
                padded[..., 2 - i : 2 - i + height, :, 2 - j : 2 - j + width],
                preferred_element_type=jnp.float32,
            )
            total = term if total is None else total + term
    return total


def plane_taps(grad_mid, rows_in, height, width):
    padded = width_pad(rows_in)
    rows_out = []
    for i in range(3):
        row_taps = []
        for j in range(3):
            row_taps.append(
                jnp.einsum(
                    "...yox,...ycx->oc",
                    grad_mid,
                    padded[..., i : i + height, :, j : j + width],
                    preferred_element_type=jnp.float32,
                )
            )
        rows_out.append(jnp.stack(row_taps))
    return jnp.stack(rows_out)


def depth_back(mix_deep, kernel, depth):
    total = None
    for k in range(3):
        term = jnp.einsum(
            "oc,zyox->zycx",
            kernel[k],
            mix_deep[2 - k : 2 - k + depth],
            preferred_element_type=jnp.float32,
        )
        total = term if total is None else total + term
    return total


def depth_taps(grad_mix, deep, depth):
    return jnp.stack(
        [
            jnp.einsum(
                "zyox,zycx->oc", grad_mix, deep[k : k + depth], preferred_element_type=jnp.float32
            )
            for k in range(3)
        ]
    )


def silu_slope(value):
    sig = jax.nn.sigmoid(value)
    return sig * (1.0 + value * (1.0 - sig))


def local(acts, grad_out, w_plane, w_depth, tiles):
    sections = acts.shape[1]
    height = acts.shape[2]
    width = acts.shape[4]
    chans = w_plane.shape[3]
    count = lax.axis_size("segment")
    layers = count * acts.shape[0]
    zs = grad_out.shape[0]
    scale = 1.0 / math.sqrt(sections * height * lax.axis_size("gy") * width)
    segment = lax.axis_index("segment")

    block = acts[0].reshape(count, -1, width)
    kernels = jnp.concatenate([w_plane.reshape(-1), w_depth.reshape(-1)]).reshape(-1, width)
    send = jnp.concatenate([block, jnp.broadcast_to(kernels[None], (count,) + kernels.shape)], axis=1)
    got = lax.all_to_all(send, "segment", 0, 0, tiled=True)
    cut_a = block.shape[1]
    mine = got[:, :cut_a].reshape((count, zs) + acts.shape[2:])
    taps = w_plane.shape[1] * w_plane.shape[2]
    weights = lax.optimization_barrier(got[:, cut_a:].reshape(count, -1, chans, chans))
    plane_w = weights[:, :taps].reshape((count,) + w_plane.shape[1:])
    depth_w = weights[:, taps:].reshape((count,) + w_depth.shape[1:])

    ids = (segment * zs + jnp.arange(zs, dtype=jnp.int32))[:, None] * (width // TILE) + jnp.arange(
        width // TILE, dtype=jnp.int32
    )[None, :]
    hit = jnp.any(tiles[0][None, None, :] == ids[:, :, None], axis=2)
    mask_full = jnp.repeat(hit.astype(jnp.float32), TILE, axis=1)[:, None, None, :]

    rows_own = padded_2(mine, (("gy", 2),), 1)
    mid = plane_conv_all(rows_own, plane_w, height, width).astype(jnp.bfloat16)
    deep = padded_2(mid, (("segment", 1),), 1)
    value = depth_conv_all(deep, depth_w, zs)
    factor = silu_slope(value) * mask_full[None]

    need = halo_plan(layers, HALO)
    reach = -(-max(need) // height)
    factor_b = factor.astype(jnp.bfloat16)
    lows, highs, picks = {}, {}, {}
    for dist in range(1, reach + 1):
        chosen = [layer for layer in range(layers) if need[layer] > height * (dist - 1)]
        picks[dist] = chosen
        load = jnp.stack([factor_b[layer] for layer in chosen] + [grad_out])
        lows[dist] = passed_along(load, "gy", dist)
        highs[dist] = passed_along(load, "gy", -dist)

    def halo_of(index_of, h, own):
        span = -(-h // height)
        low = jnp.concatenate([index_of(lows[d], d) for d in range(span, 0, -1)], axis=1)[:, -h:]
        high = jnp.concatenate([index_of(highs[d], d) for d in range(1, span + 1)], axis=1)[:, :h]
        return low, high

    def refreshed(grad, h):
        span = -(-h // height)
        low = jnp.concatenate([passed_along(grad, "gy", d) for d in range(span, 0, -1)], axis=1)
        high = jnp.concatenate([passed_along(grad, "gy", -d) for d in range(1, span + 1)], axis=1)
        return jnp.concatenate([low[:, low.shape[1] - h :], grad, high[:, :h]], axis=1)

    low, high = halo_of(lambda part, d: part[-1], need[layers - 1], grad_out)
    grad = jnp.concatenate([low, grad_out, high], axis=1)
    plane_list = [None] * layers
    depth_list = [None] * layers
    for layer in reversed(range(layers)):
        h = need[layer]
        if grad.shape[1] != height + 2 * h:
            grad = refreshed(grad, h)
        low, high = halo_of(lambda part, d: part[picks[d].index(layer)], h, None)
        wide = jnp.concatenate([low.astype(jnp.float32), factor[layer], high.astype(jnp.float32)], axis=1)
        grad_mix = (grad.astype(jnp.float32) * wide).astype(jnp.bfloat16)
        mix_deep = padded_2(grad_mix, (("segment", 0),), 1)
        grad_mid = depth_back(mix_deep, depth_w[layer], zs).astype(jnp.bfloat16)
        rows = grad.shape[1] - 2
        grad = (
            grad[:, 1:-1].astype(jnp.float32) + plane_back(grad_mid, plane_w[layer], rows, width)
        ).astype(jnp.bfloat16)
        depth_list[layer] = grad_mix[:, h : h + height]
        plane_list[layer] = grad_mid[:, h : h + height]

    wide_rows = width_pad(rows_own)

    def kernel_grads(chosen):
        mids = jnp.stack([plane_list[layer] for layer in chosen])
        mixes = jnp.stack([depth_list[layer] for layer in chosen])
        rows = wide_rows[chosen[0] : chosen[-1] + 1]
        shifted = jnp.concatenate(
            [rows[:, :, i : i + height, :, j : j + width] for i in range(3) for j in range(3)],
            axis=3,
        )
        planes = jnp.einsum("lzyox,lzykx->lok", mids, shifted, preferred_element_type=jnp.float32)
        planes = planes.reshape(len(chosen), chans, 9, chans).transpose(0, 2, 1, 3)
        deeps = deep[chosen[0] : chosen[-1] + 1]
        stacked = jnp.concatenate([deeps[:, k : k + zs] for k in range(3)], axis=3)
        depths = jnp.einsum("lzyox,lzykx->lok", mixes, stacked, preferred_element_type=jnp.float32)
        depths = depths.reshape(len(chosen), chans, 3, chans).transpose(0, 2, 1, 3)
        return planes.reshape(len(chosen), -1), depths.reshape(len(chosen), -1)

    first_p, first_d = kernel_grads([0])
    rest_p, rest_d = kernel_grads(list(range(1, layers)))
    planes = jnp.concatenate([first_p, rest_p])
    depths = jnp.concatenate([first_d, rest_d])
    flat = jnp.concatenate([planes, depths], axis=1) * scale
    spread_n = lax.axis_size("gy")
    size = flat.shape[1]
    piece = -(-size // spread_n)
    flat = jnp.pad(flat, ((0, 0), (0, piece * spread_n - size))).reshape(layers * spread_n, piece)
    part = lax.all_to_all(flat, ("segment", "gy"), 0, 0, tiled=True).sum(axis=0)
    whole = lax.all_to_all(jnp.broadcast_to(part, (spread_n, piece)), "gy", 0, 0, tiled=True)
    flat = whole.reshape(-1)[:size][None]
    cut = planes.shape[1]
    plane_sum = flat[:, :cut].reshape(-1, 3, 3, chans, chans)
    depth_sum = flat[:, cut:].reshape(-1, 3, chans, chans)
    return (grad, plane_sum, depth_sum)


def solution(mesh):
    placed = (
        P("segment", None, "gy", None, None),
        P("segment", "gy", None, None),
        P("segment", None, None, None, None),
        P("segment", None, None, None),
        P("gy", None),
    )
    return jax.shard_map(
        local,
        mesh=mesh,
        in_specs=placed,
        out_specs=(
            P("segment", "gy", None, None),
            P("segment", None, None, None, None),
            P("segment", None, None, None),
        ),
        check_vma=False,
    )
```

```python
import math

import jax
import jax.numpy as jnp
from jax import lax
from jax.sharding import PartitionSpec as P

TILE = 128
HALO = 4


def padded_2(block, sides, width):
    for axis, dim in sides:
        count = lax.axis_size(axis)
        forward = [(i, i + 1) for i in range(count - 1)]
        backward = [(target, source) for source, target in forward]
        low = lax.ppermute(
            lax.slice_in_dim(block, block.shape[dim] - width, None, axis=dim), axis, forward
        )
        high = lax.ppermute(lax.slice_in_dim(block, 0, width, axis=dim), axis, backward)
        block = jnp.concatenate([low, block, high], axis=dim)
    return block


def passed_along(block, axis, distance):
    devices = range(lax.axis_size(axis))
    route = [(i - distance, i) for i in devices if i - distance in devices]
    return lax.ppermute(block, axis, route)


def halo_plan(layers, depth):
    need = [0] * layers
    left = 0
    for layer in reversed(range(layers)):
        if left == 0:
            left = min(depth, layer + 1)
        need[layer] = left
        left -= 1
    return need


def width_pad(field):
    return jnp.pad(field, [(0, 0)] * (field.ndim - 1) + [(1, 1)])


def plane_conv_all(rows_in, kernel, height, width):
    padded = width_pad(rows_in)
    total = None
    for i in range(3):
        for j in range(3):
            term = jnp.einsum(
                "loc,lzycx->lzyox",
                kernel[:, i, j],
                padded[:, :, i : i + height, :, j : j + width],
                preferred_element_type=jnp.float32,
            )
            total = term if total is None else total + term
    return total


def depth_conv_all(deep, kernel, depth):
    total = None
    for k in range(3):
        term = jnp.einsum(
            "loc,lzycx->lzyox", kernel[:, k], deep[:, k : k + depth], preferred_element_type=jnp.float32
        )
        total = term if total is None else total + term
    return total


def plane_back(rows_grad, kernel, height, width):
    padded = width_pad(rows_grad)
    total = None
    for i in range(3):
        for j in range(3):
            term = jnp.einsum(
                "oc,...yox->...ycx",
                kernel[i, j],
                padded[..., 2 - i : 2 - i + height, :, 2 - j : 2 - j + width],
                preferred_element_type=jnp.float32,
            )
            total = term if total is None else total + term
    return total


def plane_taps(grad_mid, rows_in, height, width):
    padded = width_pad(rows_in)
    rows_out = []
    for i in range(3):
        row_taps = []
        for j in range(3):
            row_taps.append(
                jnp.einsum(
                    "...yox,...ycx->oc",
                    grad_mid,
                    padded[..., i : i + height, :, j : j + width],
                    preferred_element_type=jnp.float32,
                )
            )
        rows_out.append(jnp.stack(row_taps))
    return jnp.stack(rows_out)


def depth_back(mix_deep, kernel, depth):
    total = None
    for k in range(3):
        term = jnp.einsum(
            "oc,zyox->zycx",
            kernel[k],
            mix_deep[2 - k : 2 - k + depth],
            preferred_element_type=jnp.float32,
        )
        total = term if total is None else total + term
    return total


def depth_taps(grad_mix, deep, depth):
    return jnp.stack(
        [
            jnp.einsum(
                "zyox,zycx->oc", grad_mix, deep[k : k + depth], preferred_element_type=jnp.float32
            )
            for k in range(3)
        ]
    )


def silu_slope(value):
    sig = jax.nn.sigmoid(value)
    return sig * (1.0 + value * (1.0 - sig))


def local(acts, grad_out, w_plane, w_depth, tiles):
    sections = acts.shape[1]
    height = acts.shape[2]
    width = acts.shape[4]
    chans = w_plane.shape[3]
    count = lax.axis_size("segment")
    layers = count * acts.shape[0]
    zs = grad_out.shape[0]
    scale = 1.0 / math.sqrt(sections * height * lax.axis_size("gy") * width)
    segment = lax.axis_index("segment")

    framed = jnp.pad(acts[0], [(1, 1)] + [(0, 0)] * (acts.ndim - 2))
    block = jnp.stack([framed[d * zs : d * zs + zs + 2] for d in range(count)]).reshape(count, -1, width)
    kernels = jnp.concatenate([w_plane.reshape(-1), w_depth.reshape(-1)]).reshape(-1, width)
    send = jnp.concatenate([block, jnp.broadcast_to(kernels[None], (count,) + kernels.shape)], axis=1)
    got = lax.all_to_all(send, "segment", 0, 0, tiled=True)
    cut_a = block.shape[1]
    mine = got[:, :cut_a].reshape((count, zs + 2) + acts.shape[2:])
    taps = w_plane.shape[1] * w_plane.shape[2]
    weights = lax.optimization_barrier(got[:, cut_a:].reshape(count, -1, chans, chans))
    plane_w = weights[:, :taps].reshape((count,) + w_plane.shape[1:])
    depth_w = weights[:, taps:].reshape((count,) + w_depth.shape[1:])

    ids = (segment * zs + jnp.arange(zs, dtype=jnp.int32))[:, None] * (width // TILE) + jnp.arange(
        width // TILE, dtype=jnp.int32
    )[None, :]
    hit = jnp.any(tiles[0][None, None, :] == ids[:, :, None], axis=2)
    mask_full = jnp.repeat(hit.astype(jnp.float32), TILE, axis=1)[:, None, None, :]

    rows_all = padded_2(mine, (("gy", 2),), 1)
    deep = plane_conv_all(rows_all, plane_w, height, width).astype(jnp.bfloat16)
    rows_own = rows_all[:, 1 : 1 + zs]
    value = depth_conv_all(deep, depth_w, zs)
    factor = silu_slope(value) * mask_full[None]

    need = halo_plan(layers, HALO)
    reach = -(-max(need) // height)
    factor_b = factor.astype(jnp.bfloat16)
    lows, highs, picks = {}, {}, {}
    for dist in range(1, reach + 1):
        chosen = [layer for layer in range(layers) if need[layer] > height * (dist - 1)]
        picks[dist] = chosen
        load = jnp.stack([factor_b[layer] for layer in chosen] + [grad_out])
        lows[dist] = passed_along(load, "gy", dist)
        highs[dist] = passed_along(load, "gy", -dist)

    def halo_of(index_of, h, own):
        span = -(-h // height)
        low = jnp.concatenate([index_of(lows[d], d) for d in range(span, 0, -1)], axis=1)[:, -h:]
        high = jnp.concatenate([index_of(highs[d], d) for d in range(1, span + 1)], axis=1)[:, :h]
        return low, high

    def refreshed(grad, h):
        span = -(-h // height)
        low = jnp.concatenate([passed_along(grad, "gy", d) for d in range(span, 0, -1)], axis=1)
        high = jnp.concatenate([passed_along(grad, "gy", -d) for d in range(1, span + 1)], axis=1)
        return jnp.concatenate([low[:, low.shape[1] - h :], grad, high[:, :h]], axis=1)

    low, high = halo_of(lambda part, d: part[-1], need[layers - 1], grad_out)
    grad = jnp.concatenate([low, grad_out, high], axis=1)
    plane_list = [None] * layers
    depth_list = [None] * layers
    for layer in reversed(range(layers)):
        h = need[layer]
        if grad.shape[1] != height + 2 * h:
            grad = refreshed(grad, h)
        low, high = halo_of(lambda part, d: part[picks[d].index(layer)], h, None)
        wide = jnp.concatenate([low.astype(jnp.float32), factor[layer], high.astype(jnp.float32)], axis=1)
        grad_mix = (grad.astype(jnp.float32) * wide).astype(jnp.bfloat16)
        mix_deep = padded_2(grad_mix, (("segment", 0),), 1)
        grad_mid = depth_back(mix_deep, depth_w[layer], zs).astype(jnp.bfloat16)
        rows = grad.shape[1] - 2
        grad = (
            grad[:, 1:-1].astype(jnp.float32) + plane_back(grad_mid, plane_w[layer], rows, width)
        ).astype(jnp.bfloat16)
        depth_list[layer] = grad_mix[:, h : h + height]
        plane_list[layer] = grad_mid[:, h : h + height]

    wide_rows = width_pad(rows_own)

    def kernel_grads(chosen):
        mids = jnp.stack([plane_list[layer] for layer in chosen])
        mixes = jnp.stack([depth_list[layer] for layer in chosen])
        rows = wide_rows[chosen[0] : chosen[-1] + 1]
        shifted = jnp.concatenate(
            [rows[:, :, i : i + height, :, j : j + width] for i in range(3) for j in range(3)],
            axis=3,
        )
        planes = jnp.einsum("lzyox,lzykx->lok", mids, shifted, preferred_element_type=jnp.float32)
        planes = planes.reshape(len(chosen), chans, 9, chans).transpose(0, 2, 1, 3)
        deeps = deep[chosen[0] : chosen[-1] + 1]
        stacked = jnp.concatenate([deeps[:, k : k + zs] for k in range(3)], axis=3)
        depths = jnp.einsum("lzyox,lzykx->lok", mixes, stacked, preferred_element_type=jnp.float32)
        depths = depths.reshape(len(chosen), chans, 3, chans).transpose(0, 2, 1, 3)
        return planes.reshape(len(chosen), -1), depths.reshape(len(chosen), -1)

    first_p, first_d = kernel_grads([0])
    rest_p, rest_d = kernel_grads(list(range(1, layers)))
    planes = jnp.concatenate([first_p, rest_p])
    depths = jnp.concatenate([first_d, rest_d])
    flat = jnp.concatenate([planes, depths], axis=1) * scale
    spread_n = lax.axis_size("gy")
    size = flat.shape[1]
    piece = -(-size // spread_n)
    flat = jnp.pad(flat, ((0, 0), (0, piece * spread_n - size))).reshape(layers * spread_n, piece)
    part = lax.all_to_all(flat, ("segment", "gy"), 0, 0, tiled=True).sum(axis=0)
    whole = lax.all_to_all(jnp.broadcast_to(part, (spread_n, piece)), "gy", 0, 0, tiled=True)
    flat = whole.reshape(-1)[:size][None]
    cut = planes.shape[1]
    plane_sum = flat[:, :cut].reshape(-1, 3, 3, chans, chans)
    depth_sum = flat[:, cut:].reshape(-1, 3, chans, chans)
    return (grad, plane_sum, depth_sum)


def solution(mesh):
    placed = (
        P("segment", None, "gy", None, None),
        P("segment", "gy", None, None),
        P("segment", None, None, None, None),
        P("segment", None, None, None),
        P("gy", None),
    )
    return jax.shard_map(
        local,
        mesh=mesh,
        in_specs=placed,
        out_specs=(
            P("segment", "gy", None, None),
            P("segment", None, None, None, None),
            P("segment", None, None, None),
        ),
        check_vma=False,
    )
```

```python
import math

import jax
import jax.numpy as jnp
from jax import lax
from jax.sharding import PartitionSpec as P

TILE = 128
HALO = 4


def padded_2(block, sides, width):
    for axis, dim in sides:
        count = lax.axis_size(axis)
        forward = [(i, i + 1) for i in range(count - 1)]
        backward = [(target, source) for source, target in forward]
        low = lax.ppermute(
            lax.slice_in_dim(block, block.shape[dim] - width, None, axis=dim), axis, forward
        )
        high = lax.ppermute(lax.slice_in_dim(block, 0, width, axis=dim), axis, backward)
        block = jnp.concatenate([low, block, high], axis=dim)
    return block


def passed_along(block, axis, distance):
    devices = range(lax.axis_size(axis))
    route = [(i - distance, i) for i in devices if i - distance in devices]
    return lax.ppermute(block, axis, route)


def halo_plan(layers, depth):
    need = [0] * layers
    left = 0
    for layer in reversed(range(layers)):
        if left == 0:
            left = min(depth, layer + 1)
        need[layer] = left
        left -= 1
    return need


def width_pad(field):
    return jnp.pad(field, [(0, 0)] * (field.ndim - 1) + [(1, 1)])


def plane_conv_all(rows_in, kernel, height, width):
    padded = width_pad(rows_in)
    total = None
    for i in range(3):
        for j in range(3):
            term = jnp.einsum(
                "loc,lzycx->lzyox",
                kernel[:, i, j],
                padded[:, :, i : i + height, :, j : j + width],
                preferred_element_type=jnp.float32,
            )
            total = term if total is None else total + term
    return total


def depth_conv_all(deep, kernel, depth):
    total = None
    for k in range(3):
        term = jnp.einsum(
            "loc,lzycx->lzyox", kernel[:, k], deep[:, k : k + depth], preferred_element_type=jnp.float32
        )
        total = term if total is None else total + term
    return total


def plane_back(rows_grad, kernel, height, width):
    padded = width_pad(rows_grad)
    total = None
    for i in range(3):
        for j in range(3):
            term = jnp.einsum(
                "oc,...yox->...ycx",
                kernel[i, j],
                padded[..., 2 - i : 2 - i + height, :, 2 - j : 2 - j + width],
                preferred_element_type=jnp.float32,
            )
            total = term if total is None else total + term
    return total


def plane_taps(grad_mid, rows_in, height, width):
    padded = width_pad(rows_in)
    rows_out = []
    for i in range(3):
        row_taps = []
        for j in range(3):
            row_taps.append(
                jnp.einsum(
                    "...yox,...ycx->oc",
                    grad_mid,
                    padded[..., i : i + height, :, j : j + width],
                    preferred_element_type=jnp.float32,
                )
            )
        rows_out.append(jnp.stack(row_taps))
    return jnp.stack(rows_out)


def depth_back(mix_deep, kernel, depth):
    total = None
    for k in range(3):
        term = jnp.einsum(
            "oc,zyox->zycx",
            kernel[k],
            mix_deep[2 - k : 2 - k + depth],
            preferred_element_type=jnp.float32,
        )
        total = term if total is None else total + term
    return total


def depth_taps(grad_mix, deep, depth):
    return jnp.stack(
        [
            jnp.einsum(
                "zyox,zycx->oc", grad_mix, deep[k : k + depth], preferred_element_type=jnp.float32
            )
            for k in range(3)
        ]
    )


def silu_slope(value):
    sig = jax.nn.sigmoid(value)
    return sig * (1.0 + value * (1.0 - sig))


def local(acts, grad_out, w_plane, w_depth, tiles):
    sections = acts.shape[1]
    height = acts.shape[2]
    width = acts.shape[4]
    chans = w_plane.shape[3]
    count = lax.axis_size("segment")
    layers = count * acts.shape[0]
    zs = grad_out.shape[0]
    scale = 1.0 / math.sqrt(sections * height * lax.axis_size("gy") * width)
    segment = lax.axis_index("segment")

    block = acts[0].reshape(count, -1, width)
    kernels = jnp.concatenate([w_plane.reshape(-1), w_depth.reshape(-1)]).reshape(-1, width)
    send = jnp.concatenate([block, jnp.broadcast_to(kernels[None], (count,) + kernels.shape)], axis=1)
    got = lax.all_to_all(send, "segment", 0, 0, tiled=True)
    cut_a = block.shape[1]
    mine = got[:, :cut_a].reshape((count, zs) + acts.shape[2:])
    taps = w_plane.shape[1] * w_plane.shape[2]
    weights = lax.optimization_barrier(got[:, cut_a:].reshape(count, -1, chans, chans))
    plane_w = weights[:, :taps].reshape((count,) + w_plane.shape[1:])
    depth_w = weights[:, taps:].reshape((count,) + w_depth.shape[1:])

    ids = (segment * zs + jnp.arange(zs, dtype=jnp.int32))[:, None] * (width // TILE) + jnp.arange(
        width // TILE, dtype=jnp.int32
    )[None, :]
    hit = jnp.any(tiles[0][None, None, :] == ids[:, :, None], axis=2)
    mask_full = jnp.repeat(hit.astype(jnp.float32), TILE, axis=1)[:, None, None, :]

    rows_own = padded_2(mine, (("gy", 2),), 1)
    mid = plane_conv_all(rows_own, plane_w, height, width).astype(jnp.bfloat16)
    deep = padded_2(mid, (("segment", 1),), 1)
    value = depth_conv_all(deep, depth_w, zs)
    factor = silu_slope(value) * mask_full[None]

    need = halo_plan(layers, HALO)
    reach = -(-max(need) // height)
    factor_b = factor.astype(jnp.bfloat16)
    sources = [(factor_b[layer], need[layer]) for layer in range(layers)]
    sources.append((grad_out, need[layers - 1]))
    lows, highs, spots = {}, {}, {}
    for dist in range(1, reach + 1):
        low_parts, high_parts, at = [], [], 0
        for index, (part, h) in enumerate(sources):
            k = min(height, h - height * (dist - 1))
            if k > 0:
                low_parts.append(part[:, height - k :])
                high_parts.append(part[:, :k])
                spots[(dist, index)] = (at, k)
                at += k
        lows[dist] = passed_along(jnp.concatenate(low_parts, axis=1), "gy", dist)
        highs[dist] = passed_along(jnp.concatenate(high_parts, axis=1), "gy", -dist)

    def halo_of(index, h):
        span = -(-h // height)

        def take(block, d):
            at, k = spots[(d, index)]
            return block[:, at : at + k]

        low = jnp.concatenate([take(lows[d], d) for d in range(span, 0, -1)], axis=1)
        high = jnp.concatenate([take(highs[d], d) for d in range(1, span + 1)], axis=1)
        return low, high

    def refreshed(grad, h):
        span = -(-h // height)
        low = jnp.concatenate([passed_along(grad, "gy", d) for d in range(span, 0, -1)], axis=1)
        high = jnp.concatenate([passed_along(grad, "gy", -d) for d in range(1, span + 1)], axis=1)
        return jnp.concatenate([low[:, low.shape[1] - h :], grad, high[:, :h]], axis=1)

    low, high = halo_of(layers, need[layers - 1])
    grad = jnp.concatenate([low, grad_out, high], axis=1)
    plane_list = [None] * layers
    depth_list = [None] * layers
    for layer in reversed(range(layers)):
        h = need[layer]
        if grad.shape[1] != height + 2 * h:
            grad = refreshed(grad, h)
        low, high = halo_of(layer, h)
        wide = jnp.concatenate([low.astype(jnp.float32), factor[layer], high.astype(jnp.float32)], axis=1)
        grad_mix = (grad.astype(jnp.float32) * wide).astype(jnp.bfloat16)
        mix_deep = padded_2(grad_mix, (("segment", 0),), 1)
        grad_mid = depth_back(mix_deep, depth_w[layer], zs).astype(jnp.bfloat16)
        rows = grad.shape[1] - 2
        grad = (
            grad[:, 1:-1].astype(jnp.float32) + plane_back(grad_mid, plane_w[layer], rows, width)
        ).astype(jnp.bfloat16)
        depth_list[layer] = grad_mix[:, h : h + height]
        plane_list[layer] = grad_mid[:, h : h + height]

    wide_rows = width_pad(rows_own)

    def kernel_grads(chosen):
        mids = jnp.stack([plane_list[layer] for layer in chosen])
        mixes = jnp.stack([depth_list[layer] for layer in chosen])
        rows = wide_rows[chosen[0] : chosen[-1] + 1]
        shifted = jnp.concatenate(
            [rows[:, :, i : i + height, :, j : j + width] for i in range(3) for j in range(3)],
            axis=3,
        )
        planes = jnp.einsum("lzyox,lzykx->lok", mids, shifted, preferred_element_type=jnp.float32)
        planes = planes.reshape(len(chosen), chans, 9, chans).transpose(0, 2, 1, 3)
        deeps = deep[chosen[0] : chosen[-1] + 1]
        stacked = jnp.concatenate([deeps[:, k : k + zs] for k in range(3)], axis=3)
        depths = jnp.einsum("lzyox,lzykx->lok", mixes, stacked, preferred_element_type=jnp.float32)
        depths = depths.reshape(len(chosen), chans, 3, chans).transpose(0, 2, 1, 3)
        return planes.reshape(len(chosen), -1), depths.reshape(len(chosen), -1)

    first_p, first_d = kernel_grads([0])
    rest_p, rest_d = kernel_grads(list(range(1, layers)))
    planes = jnp.concatenate([first_p, rest_p])
    depths = jnp.concatenate([first_d, rest_d])
    flat = jnp.concatenate([planes, depths], axis=1) * scale
    spread_n = lax.axis_size("gy")
    size = flat.shape[1]
    piece = -(-size // spread_n)
    flat = jnp.pad(flat, ((0, 0), (0, piece * spread_n - size))).reshape(layers * spread_n, piece)
    sent = lax.all_to_all(flat.astype(jnp.bfloat16), ("segment", "gy"), 0, 0, tiled=True)
    part = sent.astype(jnp.float32).sum(axis=0)
    whole = lax.all_to_all(jnp.broadcast_to(part, (spread_n, piece)), "gy", 0, 0, tiled=True)
    flat = whole.reshape(-1)[:size][None]
    cut = planes.shape[1]
    plane_sum = flat[:, :cut].reshape(-1, 3, 3, chans, chans)
    depth_sum = flat[:, cut:].reshape(-1, 3, chans, chans)
    return (grad, plane_sum, depth_sum)


def solution(mesh):
    placed = (
        P("segment", None, "gy", None, None),
        P("segment", "gy", None, None),
        P("segment", None, None, None, None),
        P("segment", None, None, None),
        P("gy", None),
    )
    return jax.shard_map(
        local,
        mesh=mesh,
        in_specs=placed,
        out_specs=(
            P("segment", "gy", None, None),
            P("segment", None, None, None, None),
            P("segment", None, None, None),
        ),
        check_vma=False,
    )
```

```python
import math

import jax
import jax.numpy as jnp
from jax import lax
from jax.sharding import PartitionSpec as P

TILE = 128
HALO = 4


def padded_2(block, sides, width):
    for axis, dim in sides:
        count = lax.axis_size(axis)
        forward = [(i, i + 1) for i in range(count - 1)]
        backward = [(target, source) for source, target in forward]
        low = lax.ppermute(
            lax.slice_in_dim(block, block.shape[dim] - width, None, axis=dim), axis, forward
        )
        high = lax.ppermute(lax.slice_in_dim(block, 0, width, axis=dim), axis, backward)
        block = jnp.concatenate([low, block, high], axis=dim)
    return block


def passed_along(block, axis, distance):
    devices = range(lax.axis_size(axis))
    route = [(i - distance, i) for i in devices if i - distance in devices]
    return lax.ppermute(block, axis, route)


def halo_plan(layers, depth):
    need = [0] * layers
    left = 0
    for layer in reversed(range(layers)):
        if left == 0:
            left = min(depth, layer + 1)
        need[layer] = left
        left -= 1
    return need


def width_pad(field):
    return jnp.pad(field, [(0, 0)] * (field.ndim - 1) + [(1, 1)])


def plane_conv_all(rows_in, kernel, height, width):
    padded = width_pad(rows_in)
    total = None
    for i in range(3):
        for j in range(3):
            term = jnp.einsum(
                "loc,lzycx->lzyox",
                kernel[:, i, j],
                padded[:, :, i : i + height, :, j : j + width],
                preferred_element_type=jnp.float32,
            )
            total = term if total is None else total + term
    return total


def depth_conv_all(deep, kernel, depth):
    total = None
    for k in range(3):
        term = jnp.einsum(
            "loc,lzycx->lzyox", kernel[:, k], deep[:, k : k + depth], preferred_element_type=jnp.float32
        )
        total = term if total is None else total + term
    return total


def plane_back(rows_grad, kernel, height, width):
    padded = width_pad(rows_grad)
    total = None
    for i in range(3):
        for j in range(3):
            term = jnp.einsum(
                "oc,...yox->...ycx",
                kernel[i, j],
                padded[..., 2 - i : 2 - i + height, :, 2 - j : 2 - j + width],
                preferred_element_type=jnp.float32,
            )
            total = term if total is None else total + term
    return total


def plane_taps(grad_mid, rows_in, height, width):
    padded = width_pad(rows_in)
    rows_out = []
    for i in range(3):
        row_taps = []
        for j in range(3):
            row_taps.append(
                jnp.einsum(
                    "...yox,...ycx->oc",
                    grad_mid,
                    padded[..., i : i + height, :, j : j + width],
                    preferred_element_type=jnp.float32,
                )
            )
        rows_out.append(jnp.stack(row_taps))
    return jnp.stack(rows_out)


def depth_back(mix_deep, kernel, depth):
    total = None
    for k in range(3):
        term = jnp.einsum(
            "oc,zyox->zycx",
            kernel[k],
            mix_deep[2 - k : 2 - k + depth],
            preferred_element_type=jnp.float32,
        )
        total = term if total is None else total + term
    return total


def depth_taps(grad_mix, deep, depth):
    return jnp.stack(
        [
            jnp.einsum(
                "zyox,zycx->oc", grad_mix, deep[k : k + depth], preferred_element_type=jnp.float32
            )
            for k in range(3)
        ]
    )


def silu_slope(value):
    sig = jax.nn.sigmoid(value)
    return sig * (1.0 + value * (1.0 - sig))


def local(acts, grad_out, w_plane, w_depth, tiles):
    sections = acts.shape[1]
    height = acts.shape[2]
    width = acts.shape[4]
    chans = w_plane.shape[3]
    count = lax.axis_size("segment")
    layers = count * acts.shape[0]
    zs = grad_out.shape[0]
    scale = 1.0 / math.sqrt(sections * height * lax.axis_size("gy") * width)
    segment = lax.axis_index("segment")

    block = acts[0].reshape(count, -1, width)
    kernels = jnp.concatenate([w_plane.reshape(-1), w_depth.reshape(-1)]).reshape(-1, width)
    send = jnp.concatenate([block, jnp.broadcast_to(kernels[None], (count,) + kernels.shape)], axis=1)
    got = lax.all_to_all(send, "segment", 0, 0, tiled=True)
    cut_a = block.shape[1]
    mine = got[:, :cut_a].reshape((count, zs) + acts.shape[2:])
    taps = w_plane.shape[1] * w_plane.shape[2]
    weights = lax.optimization_barrier(got[:, cut_a:].reshape(count, -1, chans, chans))
    plane_w = weights[:, :taps].reshape((count,) + w_plane.shape[1:])
    depth_w = weights[:, taps:].reshape((count,) + w_depth.shape[1:])

    ids = (segment * zs + jnp.arange(zs, dtype=jnp.int32))[:, None] * (width // TILE) + jnp.arange(
        width // TILE, dtype=jnp.int32
    )[None, :]
    hit = jnp.any(tiles[0][None, None, :] == ids[:, :, None], axis=2)
    mask_full = jnp.repeat(hit.astype(jnp.float32), TILE, axis=1)[:, None, None, :]

    rows_own = padded_2(mine, (("gy", 2),), 1)
    mid = plane_conv_all(rows_own, plane_w, height, width).astype(jnp.bfloat16)
    deep = padded_2(mid, (("segment", 1),), 1)
    value = depth_conv_all(deep, depth_w, zs)
    factor = silu_slope(value) * mask_full[None]

    need = halo_plan(layers, HALO)
    reach = -(-max(need) // height)
    factor_b = factor.astype(jnp.bfloat16)
    lows, highs, picks = {}, {}, {}
    for dist in range(1, reach + 1):
        chosen = [layer for layer in range(layers) if need[layer] > height * (dist - 1)]
        picks[dist] = chosen
        load = jnp.stack([factor_b[layer] for layer in chosen] + [grad_out])
        lows[dist] = passed_along(load, "gy", dist)
        highs[dist] = passed_along(load, "gy", -dist)

    def halo_of(index_of, h, own):
        span = -(-h // height)
        low = jnp.concatenate([index_of(lows[d], d) for d in range(span, 0, -1)], axis=1)[:, -h:]
        high = jnp.concatenate([index_of(highs[d], d) for d in range(1, span + 1)], axis=1)[:, :h]
        return low, high

    def refreshed(grad, h):
        span = -(-h // height)
        low = jnp.concatenate([passed_along(grad, "gy", d) for d in range(span, 0, -1)], axis=1)
        high = jnp.concatenate([passed_along(grad, "gy", -d) for d in range(1, span + 1)], axis=1)
        return jnp.concatenate([low[:, low.shape[1] - h :], grad, high[:, :h]], axis=1)

    low, high = halo_of(lambda part, d: part[-1], need[layers - 1], grad_out)
    grad = jnp.concatenate([low, grad_out, high], axis=1)
    plane_list = [None] * layers
    depth_list = [None] * layers
    for layer in reversed(range(layers)):
        h = need[layer]
        if grad.shape[1] != height + 2 * h:
            grad = refreshed(grad, h)
        low, high = halo_of(lambda part, d: part[picks[d].index(layer)], h, None)
        wide = jnp.concatenate([low.astype(jnp.float32), factor[layer], high.astype(jnp.float32)], axis=1)
        grad_mix = (grad.astype(jnp.float32) * wide).astype(jnp.bfloat16)
        mix_deep = padded_2(grad_mix, (("segment", 0),), 1)
        grad_mid = depth_back(mix_deep, depth_w[layer], zs).astype(jnp.bfloat16)
        rows = grad.shape[1] - 2
        grad = (
            grad[:, 1:-1].astype(jnp.float32) + plane_back(grad_mid, plane_w[layer], rows, width)
        ).astype(jnp.bfloat16)
        depth_list[layer] = grad_mix[:, h : h + height]
        plane_list[layer] = grad_mid[:, h : h + height]

    wide_rows = width_pad(rows_own)

    def kernel_grads(chosen):
        mids = jnp.stack([plane_list[layer] for layer in chosen])
        mixes = jnp.stack([depth_list[layer] for layer in chosen])
        rows = wide_rows[chosen[0] : chosen[-1] + 1]
        shifted = jnp.concatenate(
            [rows[:, :, i : i + height, :, j : j + width] for i in range(3) for j in range(3)],
            axis=3,
        )
        planes = jnp.einsum("lzyox,lzykx->lok", mids, shifted, preferred_element_type=jnp.float32)
        planes = planes.reshape(len(chosen), chans, 9, chans).transpose(0, 2, 1, 3)
        deeps = deep[chosen[0] : chosen[-1] + 1]
        stacked = jnp.concatenate([deeps[:, k : k + zs] for k in range(3)], axis=3)
        depths = jnp.einsum("lzyox,lzykx->lok", mixes, stacked, preferred_element_type=jnp.float32)
        depths = depths.reshape(len(chosen), chans, 3, chans).transpose(0, 2, 1, 3)
        return planes.reshape(len(chosen), -1), depths.reshape(len(chosen), -1)

    first_p, first_d = kernel_grads([0])
    rest_p, rest_d = kernel_grads(list(range(1, layers)))
    planes = jnp.concatenate([first_p, rest_p])
    depths = jnp.concatenate([first_d, rest_d])
    flat = jnp.concatenate([planes, depths], axis=1) * scale
    spread_n = lax.axis_size("gy")
    size = flat.shape[1]
    piece = -(-size // spread_n)
    flat = jnp.pad(flat, ((0, 0), (0, piece * spread_n - size)))
    flat = flat.reshape(layers, spread_n, piece).transpose(1, 0, 2)
    part = lax.all_to_all(flat, "gy", 0, 0, tiled=True).sum(axis=0)
    part = lax.all_to_all(part, "segment", 0, 0, tiled=True).sum(axis=0)
    whole = lax.all_to_all(jnp.broadcast_to(part, (spread_n, piece)), "gy", 0, 0, tiled=True)
    flat = whole.reshape(-1)[:size][None]
    cut = planes.shape[1]
    plane_sum = flat[:, :cut].reshape(-1, 3, 3, chans, chans)
    depth_sum = flat[:, cut:].reshape(-1, 3, chans, chans)
    return (grad, plane_sum, depth_sum)


def solution(mesh):
    placed = (
        P("segment", None, "gy", None, None),
        P("segment", "gy", None, None),
        P("segment", None, None, None, None),
        P("segment", None, None, None),
        P("gy", None),
    )
    return jax.shard_map(
        local,
        mesh=mesh,
        in_specs=placed,
        out_specs=(
            P("segment", "gy", None, None),
            P("segment", None, None, None, None),
            P("segment", None, None, None),
        ),
        check_vma=False,
    )
```

```python
import math

import jax
import jax.numpy as jnp
from jax import lax
from jax.sharding import PartitionSpec as P

TILE = 128
HALO = 4


def padded_2(block, sides, width):
    for axis, dim in sides:
        count = lax.axis_size(axis)
        forward = [(i, i + 1) for i in range(count - 1)]
        backward = [(target, source) for source, target in forward]
        low = lax.ppermute(
            lax.slice_in_dim(block, block.shape[dim] - width, None, axis=dim), axis, forward
        )
        high = lax.ppermute(lax.slice_in_dim(block, 0, width, axis=dim), axis, backward)
        block = jnp.concatenate([low, block, high], axis=dim)
    return block


def passed_along(block, axis, distance):
    devices = range(lax.axis_size(axis))
    route = [(i - distance, i) for i in devices if i - distance in devices]
    return lax.ppermute(block, axis, route)


def halo_plan(layers, depth):
    need = [0] * layers
    left = 0
    for layer in reversed(range(layers)):
        if left == 0:
            left = min(depth, layer + 1)
        need[layer] = left
        left -= 1
    return need


def width_pad(field):
    return jnp.pad(field, [(0, 0)] * (field.ndim - 1) + [(1, 1)])


def plane_conv_all(rows_in, kernel, height, width):
    padded = width_pad(rows_in)
    total = None
    for i in range(3):
        for j in range(3):
            term = jnp.einsum(
                "loc,lzycx->lzyox",
                kernel[:, i, j],
                padded[:, :, i : i + height, :, j : j + width],
                preferred_element_type=jnp.float32,
            )
            total = term if total is None else total + term
    return total


def depth_conv_all(deep, kernel, depth):
    total = None
    for k in range(3):
        term = jnp.einsum(
            "loc,lzycx->lzyox", kernel[:, k], deep[:, k : k + depth], preferred_element_type=jnp.float32
        )
        total = term if total is None else total + term
    return total


def plane_back(rows_grad, kernel, height, width):
    padded = width_pad(rows_grad)
    stacked = jnp.concatenate(
        [
            padded[..., 2 - i : 2 - i + height, :, 2 - j : 2 - j + width]
            for i in range(3)
            for j in range(3)
        ],
        axis=-2,
    )
    flat = kernel.reshape(-1, kernel.shape[-1])
    return jnp.einsum("kc,...ykx->...ycx", flat, stacked, preferred_element_type=jnp.float32)


def plane_taps(grad_mid, rows_in, height, width):
    padded = width_pad(rows_in)
    rows_out = []
    for i in range(3):
        row_taps = []
        for j in range(3):
            row_taps.append(
                jnp.einsum(
                    "...yox,...ycx->oc",
                    grad_mid,
                    padded[..., i : i + height, :, j : j + width],
                    preferred_element_type=jnp.float32,
                )
            )
        rows_out.append(jnp.stack(row_taps))
    return jnp.stack(rows_out)


def depth_back(mix_deep, kernel, depth):
    stacked = jnp.concatenate([mix_deep[2 - k : 2 - k + depth] for k in range(3)], axis=-2)
    flat = kernel.reshape(-1, kernel.shape[-1])
    return jnp.einsum("kc,zykx->zycx", flat, stacked, preferred_element_type=jnp.float32)


def depth_taps(grad_mix, deep, depth):
    return jnp.stack(
        [
            jnp.einsum(
                "zyox,zycx->oc", grad_mix, deep[k : k + depth], preferred_element_type=jnp.float32
            )
            for k in range(3)
        ]
    )


def silu_slope(value):
    sig = jax.nn.sigmoid(value)
    return sig * (1.0 + value * (1.0 - sig))


def local(acts, grad_out, w_plane, w_depth, tiles):
    sections = acts.shape[1]
    height = acts.shape[2]
    width = acts.shape[4]
    chans = w_plane.shape[3]
    count = lax.axis_size("segment")
    layers = count * acts.shape[0]
    zs = grad_out.shape[0]
    scale = 1.0 / math.sqrt(sections * height * lax.axis_size("gy") * width)
    segment = lax.axis_index("segment")

    block = acts[0].reshape(count, -1, width)
    kernels = jnp.concatenate([w_plane.reshape(-1), w_depth.reshape(-1)]).reshape(-1, width)
    send = jnp.concatenate([block, jnp.broadcast_to(kernels[None], (count,) + kernels.shape)], axis=1)
    got = lax.all_to_all(send, "segment", 0, 0, tiled=True)
    cut_a = block.shape[1]
    mine = got[:, :cut_a].reshape((count, zs) + acts.shape[2:])
    taps = w_plane.shape[1] * w_plane.shape[2]
    weights = lax.optimization_barrier(got[:, cut_a:].reshape(count, -1, chans, chans))
    plane_w = weights[:, :taps].reshape((count,) + w_plane.shape[1:])
    depth_w = weights[:, taps:].reshape((count,) + w_depth.shape[1:])

    ids = (segment * zs + jnp.arange(zs, dtype=jnp.int32))[:, None] * (width // TILE) + jnp.arange(
        width // TILE, dtype=jnp.int32
    )[None, :]
    hit = jnp.any(tiles[0][None, None, :] == ids[:, :, None], axis=2)
    mask_full = jnp.repeat(hit.astype(jnp.float32), TILE, axis=1)[:, None, None, :]

    rows_own = padded_2(mine, (("gy", 2),), 1)
    mid = plane_conv_all(rows_own, plane_w, height, width).astype(jnp.bfloat16)
    deep = padded_2(mid, (("segment", 1),), 1)
    value = depth_conv_all(deep, depth_w, zs)
    factor = silu_slope(value) * mask_full[None]

    need = halo_plan(layers, HALO)
    reach = -(-max(need) // height)
    factor_b = factor.astype(jnp.bfloat16)
    lows, highs, picks = {}, {}, {}
    for dist in range(1, reach + 1):
        chosen = [layer for layer in range(layers) if need[layer] > height * (dist - 1)]
        picks[dist] = chosen
        load = jnp.stack([factor_b[layer] for layer in chosen] + [grad_out])
        lows[dist] = passed_along(load, "gy", dist)
        highs[dist] = passed_along(load, "gy", -dist)

    def halo_of(index_of, h, own):
        span = -(-h // height)
        low = jnp.concatenate([index_of(lows[d], d) for d in range(span, 0, -1)], axis=1)[:, -h:]
        high = jnp.concatenate([index_of(highs[d], d) for d in range(1, span + 1)], axis=1)[:, :h]
        return low, high

    def refreshed(grad, h):
        span = -(-h // height)
        low = jnp.concatenate([passed_along(grad, "gy", d) for d in range(span, 0, -1)], axis=1)
        high = jnp.concatenate([passed_along(grad, "gy", -d) for d in range(1, span + 1)], axis=1)
        return jnp.concatenate([low[:, low.shape[1] - h :], grad, high[:, :h]], axis=1)

    low, high = halo_of(lambda part, d: part[-1], need[layers - 1], grad_out)
    grad = jnp.concatenate([low, grad_out, high], axis=1)
    plane_list = [None] * layers
    depth_list = [None] * layers
    for layer in reversed(range(layers)):
        h = need[layer]
        if grad.shape[1] != height + 2 * h:
            grad = refreshed(grad, h)
        low, high = halo_of(lambda part, d: part[picks[d].index(layer)], h, None)
        wide = jnp.concatenate([low.astype(jnp.float32), factor[layer], high.astype(jnp.float32)], axis=1)
        grad_mix = (grad.astype(jnp.float32) * wide).astype(jnp.bfloat16)
        mix_deep = padded_2(grad_mix, (("segment", 0),), 1)
        grad_mid = depth_back(mix_deep, depth_w[layer], zs).astype(jnp.bfloat16)
        rows = grad.shape[1] - 2
        grad = (
            grad[:, 1:-1].astype(jnp.float32) + plane_back(grad_mid, plane_w[layer], rows, width)
        ).astype(jnp.bfloat16)
        depth_list[layer] = grad_mix[:, h : h + height]
        plane_list[layer] = grad_mid[:, h : h + height]

    wide_rows = width_pad(rows_own)

    def kernel_grads(chosen):
        mids = jnp.stack([plane_list[layer] for layer in chosen])
        mixes = jnp.stack([depth_list[layer] for layer in chosen])
        rows = wide_rows[chosen[0] : chosen[-1] + 1]
        shifted = jnp.concatenate(
            [rows[:, :, i : i + height, :, j : j + width] for i in range(3) for j in range(3)],
            axis=3,
        )
        planes = jnp.einsum("lzyox,lzykx->lok", mids, shifted, preferred_element_type=jnp.float32)
        planes = planes.reshape(len(chosen), chans, 9, chans).transpose(0, 2, 1, 3)
        deeps = deep[chosen[0] : chosen[-1] + 1]
        stacked = jnp.concatenate([deeps[:, k : k + zs] for k in range(3)], axis=3)
        depths = jnp.einsum("lzyox,lzykx->lok", mixes, stacked, preferred_element_type=jnp.float32)
        depths = depths.reshape(len(chosen), chans, 3, chans).transpose(0, 2, 1, 3)
        return planes.reshape(len(chosen), -1), depths.reshape(len(chosen), -1)

    first_p, first_d = kernel_grads([0])
    rest_p, rest_d = kernel_grads(list(range(1, layers)))
    planes = jnp.concatenate([first_p, rest_p])
    depths = jnp.concatenate([first_d, rest_d])
    flat = jnp.concatenate([planes, depths], axis=1) * scale
    spread_n = lax.axis_size("gy")
    size = flat.shape[1]
    piece = -(-size // spread_n)
    flat = jnp.pad(flat, ((0, 0), (0, piece * spread_n - size))).reshape(layers * spread_n, piece)
    part = lax.all_to_all(flat, ("segment", "gy"), 0, 0, tiled=True).sum(axis=0)
    whole = lax.all_to_all(jnp.broadcast_to(part, (spread_n, piece)), "gy", 0, 0, tiled=True)
    flat = whole.reshape(-1)[:size][None]
    cut = planes.shape[1]
    plane_sum = flat[:, :cut].reshape(-1, 3, 3, chans, chans)
    depth_sum = flat[:, cut:].reshape(-1, 3, chans, chans)
    return (grad, plane_sum, depth_sum)


def solution(mesh):
    placed = (
        P("segment", None, "gy", None, None),
        P("segment", "gy", None, None),
        P("segment", None, None, None, None),
        P("segment", None, None, None),
        P("gy", None),
    )
    return jax.shard_map(
        local,
        mesh=mesh,
        in_specs=placed,
        out_specs=(
            P("segment", "gy", None, None),
            P("segment", None, None, None, None),
            P("segment", None, None, None),
        ),
        check_vma=False,
    )
```

```python
import math

import jax
import jax.numpy as jnp
from jax import lax
from jax.sharding import PartitionSpec as P

TILE = 128
HALO = 4


def padded_2(block, sides, width):
    for axis, dim in sides:
        count = lax.axis_size(axis)
        forward = [(i, i + 1) for i in range(count - 1)]
        backward = [(target, source) for source, target in forward]
        low = lax.ppermute(
            lax.slice_in_dim(block, block.shape[dim] - width, None, axis=dim), axis, forward
        )
        high = lax.ppermute(lax.slice_in_dim(block, 0, width, axis=dim), axis, backward)
        block = jnp.concatenate([low, block, high], axis=dim)
    return block


def passed_along(block, axis, distance):
    devices = range(lax.axis_size(axis))
    route = [(i - distance, i) for i in devices if i - distance in devices]
    return lax.ppermute(block, axis, route)


def halo_plan(layers, depth):
    need = [0] * layers
    left = 0
    for layer in reversed(range(layers)):
        if left == 0:
            left = min(depth, layer + 1)
        need[layer] = left
        left -= 1
    return need


def width_pad(field):
    return jnp.pad(field, [(0, 0)] * (field.ndim - 1) + [(1, 1)])


def plane_conv_all(rows_in, kernel, height, width):
    padded = width_pad(rows_in)
    stacked = jnp.concatenate(
        [padded[:, :, i : i + height, :, j : j + width] for i in range(3) for j in range(3)],
        axis=-2,
    )
    flat = kernel.reshape((kernel.shape[0], 9) + kernel.shape[3:]).transpose(0, 2, 1, 3)
    flat = flat.reshape(kernel.shape[0], kernel.shape[3], -1)
    return jnp.einsum("lok,lzykx->lzyox", flat, stacked, preferred_element_type=jnp.float32)


def depth_conv_all(deep, kernel, depth):
    stacked = jnp.concatenate([deep[:, k : k + depth] for k in range(3)], axis=-2)
    flat = kernel.transpose(0, 2, 1, 3).reshape(kernel.shape[0], kernel.shape[2], -1)
    return jnp.einsum("lok,lzykx->lzyox", flat, stacked, preferred_element_type=jnp.float32)


def plane_back(rows_grad, kernel, height, width):
    padded = width_pad(rows_grad)
    stacked = jnp.concatenate(
        [
            padded[..., 2 - i : 2 - i + height, :, 2 - j : 2 - j + width]
            for i in range(3)
            for j in range(3)
        ],
        axis=-2,
    )
    flat = kernel.reshape(-1, kernel.shape[-1])
    return jnp.einsum("kc,...ykx->...ycx", flat, stacked, preferred_element_type=jnp.float32)


def plane_taps(grad_mid, rows_in, height, width):
    padded = width_pad(rows_in)
    rows_out = []
    for i in range(3):
        row_taps = []
        for j in range(3):
            row_taps.append(
                jnp.einsum(
                    "...yox,...ycx->oc",
                    grad_mid,
                    padded[..., i : i + height, :, j : j + width],
                    preferred_element_type=jnp.float32,
                )
            )
        rows_out.append(jnp.stack(row_taps))
    return jnp.stack(rows_out)


def depth_back(mix_deep, kernel, depth):
    stacked = jnp.concatenate([mix_deep[2 - k : 2 - k + depth] for k in range(3)], axis=-2)
    flat = kernel.reshape(-1, kernel.shape[-1])
    return jnp.einsum("kc,zykx->zycx", flat, stacked, preferred_element_type=jnp.float32)


def depth_taps(grad_mix, deep, depth):
    return jnp.stack(
        [
            jnp.einsum(
                "zyox,zycx->oc", grad_mix, deep[k : k + depth], preferred_element_type=jnp.float32
            )
            for k in range(3)
        ]
    )


def silu_slope(value):
    sig = jax.nn.sigmoid(value)
    return sig * (1.0 + value * (1.0 - sig))


def local(acts, grad_out, w_plane, w_depth, tiles):
    sections = acts.shape[1]
    height = acts.shape[2]
    width = acts.shape[4]
    chans = w_plane.shape[3]
    count = lax.axis_size("segment")
    layers = count * acts.shape[0]
    zs = grad_out.shape[0]
    scale = 1.0 / math.sqrt(sections * height * lax.axis_size("gy") * width)
    segment = lax.axis_index("segment")

    block = acts[0].reshape(count, -1, width)
    kernels = jnp.concatenate([w_plane.reshape(-1), w_depth.reshape(-1)]).reshape(-1, width)
    send = jnp.concatenate([block, jnp.broadcast_to(kernels[None], (count,) + kernels.shape)], axis=1)
    got = lax.all_to_all(send, "segment", 0, 0, tiled=True)
    cut_a = block.shape[1]
    mine = got[:, :cut_a].reshape((count, zs) + acts.shape[2:])
    taps = w_plane.shape[1] * w_plane.shape[2]
    weights = lax.optimization_barrier(got[:, cut_a:].reshape(count, -1, chans, chans))
    plane_w = weights[:, :taps].reshape((count,) + w_plane.shape[1:])
    depth_w = weights[:, taps:].reshape((count,) + w_depth.shape[1:])

    ids = (segment * zs + jnp.arange(zs, dtype=jnp.int32))[:, None] * (width // TILE) + jnp.arange(
        width // TILE, dtype=jnp.int32
    )[None, :]
    hit = jnp.any(tiles[0][None, None, :] == ids[:, :, None], axis=2)
    mask_full = jnp.repeat(hit.astype(jnp.float32), TILE, axis=1)[:, None, None, :]

    rows_own = padded_2(mine, (("gy", 2),), 1)
    mid = plane_conv_all(rows_own, plane_w, height, width).astype(jnp.bfloat16)
    deep = padded_2(mid, (("segment", 1),), 1)
    value = depth_conv_all(deep, depth_w, zs)
    factor = silu_slope(value) * mask_full[None]

    need = halo_plan(layers, HALO)
    reach = -(-max(need) // height)
    factor_b = factor.astype(jnp.bfloat16)
    lows, highs, picks = {}, {}, {}
    for dist in range(1, reach + 1):
        chosen = [layer for layer in range(layers) if need[layer] > height * (dist - 1)]
        picks[dist] = chosen
        load = jnp.stack([factor_b[layer] for layer in chosen] + [grad_out])
        lows[dist] = passed_along(load, "gy", dist)
        highs[dist] = passed_along(load, "gy", -dist)

    def halo_of(index_of, h, own):
        span = -(-h // height)
        low = jnp.concatenate([index_of(lows[d], d) for d in range(span, 0, -1)], axis=1)[:, -h:]
        high = jnp.concatenate([index_of(highs[d], d) for d in range(1, span + 1)], axis=1)[:, :h]
        return low, high

    def refreshed(grad, h):
        span = -(-h // height)
        low = jnp.concatenate([passed_along(grad, "gy", d) for d in range(span, 0, -1)], axis=1)
        high = jnp.concatenate([passed_along(grad, "gy", -d) for d in range(1, span + 1)], axis=1)
        return jnp.concatenate([low[:, low.shape[1] - h :], grad, high[:, :h]], axis=1)

    low, high = halo_of(lambda part, d: part[-1], need[layers - 1], grad_out)
    grad = jnp.concatenate([low, grad_out, high], axis=1)
    plane_list = [None] * layers
    depth_list = [None] * layers
    for layer in reversed(range(layers)):
        h = need[layer]
        if grad.shape[1] != height + 2 * h:
            grad = refreshed(grad, h)
        low, high = halo_of(lambda part, d: part[picks[d].index(layer)], h, None)
        wide = jnp.concatenate([low.astype(jnp.float32), factor[layer], high.astype(jnp.float32)], axis=1)
        grad_mix = (grad.astype(jnp.float32) * wide).astype(jnp.bfloat16)
        mix_deep = padded_2(grad_mix, (("segment", 0),), 1)
        grad_mid = depth_back(mix_deep, depth_w[layer], zs).astype(jnp.bfloat16)
        rows = grad.shape[1] - 2
        grad = (
            grad[:, 1:-1].astype(jnp.float32) + plane_back(grad_mid, plane_w[layer], rows, width)
        ).astype(jnp.bfloat16)
        depth_list[layer] = grad_mix[:, h : h + height]
        plane_list[layer] = grad_mid[:, h : h + height]

    wide_rows = width_pad(rows_own)

    def kernel_grads(chosen):
        mids = jnp.stack([plane_list[layer] for layer in chosen])
        mixes = jnp.stack([depth_list[layer] for layer in chosen])
        rows = wide_rows[chosen[0] : chosen[-1] + 1]
        shifted = jnp.concatenate(
            [rows[:, :, i : i + height, :, j : j + width] for i in range(3) for j in range(3)],
            axis=3,
        )
        planes = jnp.einsum("lzyox,lzykx->lok", mids, shifted, preferred_element_type=jnp.float32)
        planes = planes.reshape(len(chosen), chans, 9, chans).transpose(0, 2, 1, 3)
        deeps = deep[chosen[0] : chosen[-1] + 1]
        stacked = jnp.concatenate([deeps[:, k : k + zs] for k in range(3)], axis=3)
        depths = jnp.einsum("lzyox,lzykx->lok", mixes, stacked, preferred_element_type=jnp.float32)
        depths = depths.reshape(len(chosen), chans, 3, chans).transpose(0, 2, 1, 3)
        return planes.reshape(len(chosen), -1), depths.reshape(len(chosen), -1)

    first_p, first_d = kernel_grads([0])
    rest_p, rest_d = kernel_grads(list(range(1, layers)))
    planes = jnp.concatenate([first_p, rest_p])
    depths = jnp.concatenate([first_d, rest_d])
    flat = jnp.concatenate([planes, depths], axis=1)
    spread_n = lax.axis_size("gy")
    size = flat.shape[1]
    piece = 128 * -(-size // (128 * spread_n))
    flat = jnp.pad(flat, ((0, 0), (0, piece * spread_n - size))).reshape(layers * spread_n, piece)
    part = lax.all_to_all(flat, ("segment", "gy"), 0, 0, tiled=True).sum(axis=0)
    whole = lax.all_to_all(jnp.broadcast_to(part, (spread_n, piece)), "gy", 0, 0, tiled=True)
    flat = whole.reshape(-1)[:size][None] * scale
    cut = planes.shape[1]
    plane_sum = flat[:, :cut].reshape(-1, 3, 3, chans, chans)
    depth_sum = flat[:, cut:].reshape(-1, 3, chans, chans)
    return (grad, plane_sum, depth_sum)


def solution(mesh):
    placed = (
        P("segment", None, "gy", None, None),
        P("segment", "gy", None, None),
        P("segment", None, None, None, None),
        P("segment", None, None, None),
        P("gy", None),
    )
    return jax.shard_map(
        local,
        mesh=mesh,
        in_specs=placed,
        out_specs=(
            P("segment", "gy", None, None),
            P("segment", None, None, None, None),
            P("segment", None, None, None),
        ),
        check_vma=False,
    )
```

```python
import math

import jax
import jax.numpy as jnp
from jax import lax
from jax.sharding import PartitionSpec as P

TILE = 128
HALO = 6


def padded_2(block, sides, width):
    for axis, dim in sides:
        count = lax.axis_size(axis)
        forward = [(i, i + 1) for i in range(count - 1)]
        backward = [(target, source) for source, target in forward]
        low = lax.ppermute(
            lax.slice_in_dim(block, block.shape[dim] - width, None, axis=dim), axis, forward
        )
        high = lax.ppermute(lax.slice_in_dim(block, 0, width, axis=dim), axis, backward)
        block = jnp.concatenate([low, block, high], axis=dim)
    return block


def passed_along(block, axis, distance):
    devices = range(lax.axis_size(axis))
    route = [(i - distance, i) for i in devices if i - distance in devices]
    return lax.ppermute(block, axis, route)


def halo_plan(layers, depth):
    need = [0] * layers
    left = 0
    for layer in reversed(range(layers)):
        if left == 0:
            left = min(depth, layer + 1)
        need[layer] = left
        left -= 1
    return need


def width_pad(field):
    return jnp.pad(field, [(0, 0)] * (field.ndim - 1) + [(1, 1)])


def plane_conv_all(rows_in, kernel, height, width):
    padded = width_pad(rows_in)
    stacked = jnp.concatenate(
        [padded[:, :, i : i + height, :, j : j + width] for i in range(3) for j in range(3)],
        axis=-2,
    )
    flat = kernel.reshape((kernel.shape[0], 9) + kernel.shape[3:]).transpose(0, 2, 1, 3)
    flat = flat.reshape(kernel.shape[0], kernel.shape[3], -1)
    return jnp.einsum("lok,lzykx->lzyox", flat, stacked, preferred_element_type=jnp.float32)


def depth_conv_all(deep, kernel, depth):
    stacked = jnp.concatenate([deep[:, k : k + depth] for k in range(3)], axis=-2)
    flat = kernel.transpose(0, 2, 1, 3).reshape(kernel.shape[0], kernel.shape[2], -1)
    return jnp.einsum("lok,lzykx->lzyox", flat, stacked, preferred_element_type=jnp.float32)


def plane_back(rows_grad, kernel, height, width):
    padded = width_pad(rows_grad)
    stacked = jnp.concatenate(
        [
            padded[..., 2 - i : 2 - i + height, :, 2 - j : 2 - j + width]
            for i in range(3)
            for j in range(3)
        ],
        axis=-2,
    )
    flat = kernel.reshape(-1, kernel.shape[-1])
    return jnp.einsum("kc,...ykx->...ycx", flat, stacked, preferred_element_type=jnp.float32)


def plane_taps(grad_mid, rows_in, height, width):
    padded = width_pad(rows_in)
    rows_out = []
    for i in range(3):
        row_taps = []
        for j in range(3):
            row_taps.append(
                jnp.einsum(
                    "...yox,...ycx->oc",
                    grad_mid,
                    padded[..., i : i + height, :, j : j + width],
                    preferred_element_type=jnp.float32,
                )
            )
        rows_out.append(jnp.stack(row_taps))
    return jnp.stack(rows_out)


def depth_back(mix_deep, kernel, depth):
    stacked = jnp.concatenate([mix_deep[2 - k : 2 - k + depth] for k in range(3)], axis=-2)
    flat = kernel.reshape(-1, kernel.shape[-1])
    return jnp.einsum("kc,zykx->zycx", flat, stacked, preferred_element_type=jnp.float32)


def depth_taps(grad_mix, deep, depth):
    return jnp.stack(
        [
            jnp.einsum(
                "zyox,zycx->oc", grad_mix, deep[k : k + depth], preferred_element_type=jnp.float32
            )
            for k in range(3)
        ]
    )


def silu_slope(value):
    sig = jax.nn.sigmoid(value)
    return sig * (1.0 + value * (1.0 - sig))


def local(acts, grad_out, w_plane, w_depth, tiles):
    sections = acts.shape[1]
    height = acts.shape[2]
    width = acts.shape[4]
    chans = w_plane.shape[3]
    count = lax.axis_size("segment")
    layers = count * acts.shape[0]
    zs = grad_out.shape[0]
    scale = 1.0 / math.sqrt(sections * height * lax.axis_size("gy") * width)
    segment = lax.axis_index("segment")

    block = acts[0].reshape(count, -1, width)
    kernels = jnp.concatenate([w_plane.reshape(-1), w_depth.reshape(-1)]).reshape(-1, width)
    send = jnp.concatenate([block, jnp.broadcast_to(kernels[None], (count,) + kernels.shape)], axis=1)
    got = lax.all_to_all(send, "segment", 0, 0, tiled=True)
    cut_a = block.shape[1]
    mine = got[:, :cut_a].reshape((count, zs) + acts.shape[2:])
    taps = w_plane.shape[1] * w_plane.shape[2]
    weights = lax.optimization_barrier(got[:, cut_a:].reshape(count, -1, chans, chans))
    plane_w = weights[:, :taps].reshape((count,) + w_plane.shape[1:])
    depth_w = weights[:, taps:].reshape((count,) + w_depth.shape[1:])

    ids = (segment * zs + jnp.arange(zs, dtype=jnp.int32))[:, None] * (width // TILE) + jnp.arange(
        width // TILE, dtype=jnp.int32
    )[None, :]
    hit = jnp.any(tiles[0][None, None, :] == ids[:, :, None], axis=2)
    mask_full = jnp.repeat(hit.astype(jnp.float32), TILE, axis=1)[:, None, None, :]

    rows_own = padded_2(mine, (("gy", 2),), 1)
    mid = plane_conv_all(rows_own, plane_w, height, width).astype(jnp.bfloat16)
    deep = padded_2(mid, (("segment", 1),), 1)
    value = depth_conv_all(deep, depth_w, zs)
    factor = silu_slope(value) * mask_full[None]

    need = halo_plan(layers, HALO)
    reach = -(-max(need) // height)
    factor_b = factor.astype(jnp.bfloat16)
    lows, highs, picks = {}, {}, {}
    for dist in range(1, reach + 1):
        chosen = [layer for layer in range(layers) if need[layer] > height * (dist - 1)]
        picks[dist] = chosen
        load = jnp.stack([factor_b[layer] for layer in chosen] + [grad_out])
        lows[dist] = passed_along(load, "gy", dist)
        highs[dist] = passed_along(load, "gy", -dist)

    def halo_of(index_of, h, own):
        span = -(-h // height)
        low = jnp.concatenate([index_of(lows[d], d) for d in range(span, 0, -1)], axis=1)[:, -h:]
        high = jnp.concatenate([index_of(highs[d], d) for d in range(1, span + 1)], axis=1)[:, :h]
        return low, high

    def refreshed(grad, h):
        span = -(-h // height)
        low = jnp.concatenate([passed_along(grad, "gy", d) for d in range(span, 0, -1)], axis=1)
        high = jnp.concatenate([passed_along(grad, "gy", -d) for d in range(1, span + 1)], axis=1)
        return jnp.concatenate([low[:, low.shape[1] - h :], grad, high[:, :h]], axis=1)

    low, high = halo_of(lambda part, d: part[-1], need[layers - 1], grad_out)
    grad = jnp.concatenate([low, grad_out, high], axis=1)
    plane_list = [None] * layers
    depth_list = [None] * layers
    for layer in reversed(range(layers)):
        h = need[layer]
        if grad.shape[1] != height + 2 * h:
            grad = refreshed(grad, h)
        low, high = halo_of(lambda part, d: part[picks[d].index(layer)], h, None)
        wide = jnp.concatenate([low.astype(jnp.float32), factor[layer], high.astype(jnp.float32)], axis=1)
        grad_mix = (grad.astype(jnp.float32) * wide).astype(jnp.bfloat16)
        mix_deep = padded_2(grad_mix, (("segment", 0),), 1)
        grad_mid = depth_back(mix_deep, depth_w[layer], zs).astype(jnp.bfloat16)
        rows = grad.shape[1] - 2
        grad = (
            grad[:, 1:-1].astype(jnp.float32) + plane_back(grad_mid, plane_w[layer], rows, width)
        ).astype(jnp.bfloat16)
        depth_list[layer] = grad_mix[:, h : h + height]
        plane_list[layer] = grad_mid[:, h : h + height]

    wide_rows = width_pad(rows_own)

    def kernel_grads(chosen):
        mids = jnp.stack([plane_list[layer] for layer in chosen])
        mixes = jnp.stack([depth_list[layer] for layer in chosen])
        rows = wide_rows[chosen[0] : chosen[-1] + 1]
        shifted = jnp.concatenate(
            [rows[:, :, i : i + height, :, j : j + width] for i in range(3) for j in range(3)],
            axis=3,
        )
        planes = jnp.einsum("lzyox,lzykx->lok", mids, shifted, preferred_element_type=jnp.float32)
        planes = planes.reshape(len(chosen), chans, 9, chans).transpose(0, 2, 1, 3)
        deeps = deep[chosen[0] : chosen[-1] + 1]
        stacked = jnp.concatenate([deeps[:, k : k + zs] for k in range(3)], axis=3)
        depths = jnp.einsum("lzyox,lzykx->lok", mixes, stacked, preferred_element_type=jnp.float32)
        depths = depths.reshape(len(chosen), chans, 3, chans).transpose(0, 2, 1, 3)
        return planes.reshape(len(chosen), -1), depths.reshape(len(chosen), -1)

    first_p, first_d = kernel_grads([0])
    rest_p, rest_d = kernel_grads(list(range(1, layers)))
    planes = jnp.concatenate([first_p, rest_p])
    depths = jnp.concatenate([first_d, rest_d])
    flat = jnp.concatenate([planes, depths], axis=1)
    spread_n = lax.axis_size("gy")
    size = flat.shape[1]
    piece = 128 * -(-size // (128 * spread_n))
    flat = jnp.pad(flat, ((0, 0), (0, piece * spread_n - size))).reshape(layers * spread_n, piece)
    part = lax.all_to_all(flat, ("segment", "gy"), 0, 0, tiled=True).sum(axis=0)
    whole = lax.all_to_all(jnp.broadcast_to(part, (spread_n, piece)), "gy", 0, 0, tiled=True)
    flat = whole.reshape(-1)[:size][None] * scale
    cut = planes.shape[1]
    plane_sum = flat[:, :cut].reshape(-1, 3, 3, chans, chans)
    depth_sum = flat[:, cut:].reshape(-1, 3, chans, chans)
    return (grad, plane_sum, depth_sum)


def solution(mesh):
    placed = (
        P("segment", None, "gy", None, None),
        P("segment", "gy", None, None),
        P("segment", None, None, None, None),
        P("segment", None, None, None),
        P("gy", None),
    )
    return jax.shard_map(
        local,
        mesh=mesh,
        in_specs=placed,
        out_specs=(
            P("segment", "gy", None, None),
            P("segment", None, None, None, None),
            P("segment", None, None, None),
        ),
        check_vma=False,
    )
```

```python
import math

import jax
import jax.numpy as jnp
from jax import lax
from jax.sharding import PartitionSpec as P

TILE = 128
HALO = 4


def padded_2(block, sides, width):
    for axis, dim in sides:
        count = lax.axis_size(axis)
        forward = [(i, i + 1) for i in range(count - 1)]
        backward = [(target, source) for source, target in forward]
        low = lax.ppermute(
            lax.slice_in_dim(block, block.shape[dim] - width, None, axis=dim), axis, forward
        )
        high = lax.ppermute(lax.slice_in_dim(block, 0, width, axis=dim), axis, backward)
        block = jnp.concatenate([low, block, high], axis=dim)
    return block


def passed_along(block, axis, distance):
    devices = range(lax.axis_size(axis))
    route = [(i - distance, i) for i in devices if i - distance in devices]
    return lax.ppermute(block, axis, route)


def halo_plan(layers, depth):
    need = [0] * layers
    left = 0
    for layer in reversed(range(layers)):
        if left == 0:
            left = min(depth, layer + 1)
        need[layer] = left
        left -= 1
    return need


def width_pad(field):
    return jnp.pad(field, [(0, 0)] * (field.ndim - 1) + [(1, 1)])


def plane_conv_all(rows_in, kernel, height, width):
    padded = width_pad(rows_in)
    stacked = jnp.concatenate(
        [padded[:, :, i : i + height, :, j : j + width] for i in range(3) for j in range(3)],
        axis=-2,
    )
    flat = kernel.reshape((kernel.shape[0], 9) + kernel.shape[3:]).transpose(0, 2, 1, 3)
    flat = flat.reshape(kernel.shape[0], kernel.shape[3], -1)
    return jnp.einsum("lok,lzykx->lzyox", flat, stacked, preferred_element_type=jnp.float32)


def depth_conv_all(deep, kernel, depth):
    stacked = jnp.concatenate([deep[:, k : k + depth] for k in range(3)], axis=-2)
    flat = kernel.transpose(0, 2, 1, 3).reshape(kernel.shape[0], kernel.shape[2], -1)
    return jnp.einsum("lok,lzykx->lzyox", flat, stacked, preferred_element_type=jnp.float32)


def plane_back(rows_grad, kernel, height, width):
    padded = width_pad(rows_grad)
    stacked = jnp.concatenate(
        [
            padded[..., 2 - i : 2 - i + height, :, 2 - j : 2 - j + width]
            for i in range(3)
            for j in range(3)
        ],
        axis=-2,
    )
    flat = kernel.reshape(-1, kernel.shape[-1])
    return jnp.einsum("kc,...ykx->...ycx", flat, stacked, preferred_element_type=jnp.float32)


def plane_taps(grad_mid, rows_in, height, width):
    padded = width_pad(rows_in)
    rows_out = []
    for i in range(3):
        row_taps = []
        for j in range(3):
            row_taps.append(
                jnp.einsum(
                    "...yox,...ycx->oc",
                    grad_mid,
                    padded[..., i : i + height, :, j : j + width],
                    preferred_element_type=jnp.float32,
                )
            )
        rows_out.append(jnp.stack(row_taps))
    return jnp.stack(rows_out)


def depth_back(mix_deep, kernel, depth):
    stacked = jnp.concatenate([mix_deep[2 - k : 2 - k + depth] for k in range(3)], axis=-2)
    flat = kernel.reshape(-1, kernel.shape[-1])
    return jnp.einsum("kc,zykx->zycx", flat, stacked, preferred_element_type=jnp.float32)


def depth_taps(grad_mix, deep, depth):
    return jnp.stack(
        [
            jnp.einsum(
                "zyox,zycx->oc", grad_mix, deep[k : k + depth], preferred_element_type=jnp.float32
            )
            for k in range(3)
        ]
    )


def silu_slope(value):
    sig = jax.nn.sigmoid(value)
    return sig * (1.0 + value * (1.0 - sig))


def local(acts, grad_out, w_plane, w_depth, tiles):
    sections = acts.shape[1]
    height = acts.shape[2]
    width = acts.shape[4]
    chans = w_plane.shape[3]
    count = lax.axis_size("segment")
    layers = count * acts.shape[0]
    zs = grad_out.shape[0]
    scale = 1.0 / math.sqrt(sections * height * lax.axis_size("gy") * width)
    segment = lax.axis_index("segment")

    block = acts[0].reshape(count, -1, width)
    kernels = jnp.concatenate([w_plane.reshape(-1), w_depth.reshape(-1)]).reshape(-1, width)
    send = jnp.concatenate([block, jnp.broadcast_to(kernels[None], (count,) + kernels.shape)], axis=1)
    got = lax.all_to_all(send, "segment", 0, 0, tiled=True)
    cut_a = block.shape[1]
    mine = got[:, :cut_a].reshape((count, zs) + acts.shape[2:])
    taps = w_plane.shape[1] * w_plane.shape[2]
    weights = lax.optimization_barrier(got[:, cut_a:].reshape(count, -1, chans, chans))
    plane_w = weights[:, :taps].reshape((count,) + w_plane.shape[1:])
    depth_w = weights[:, taps:].reshape((count,) + w_depth.shape[1:])

    ids = (segment * zs + jnp.arange(zs, dtype=jnp.int32))[:, None] * (width // TILE) + jnp.arange(
        width // TILE, dtype=jnp.int32
    )[None, :]
    hit = jnp.any(tiles[0][None, None, :] == ids[:, :, None], axis=2)
    mask_full = jnp.repeat(hit.astype(jnp.float32), TILE, axis=1)[:, None, None, :]

    rows_own = padded_2(mine, (("gy", 2),), 1)
    mid = plane_conv_all(rows_own, plane_w, height, width).astype(jnp.bfloat16)
    deep = padded_2(mid, (("segment", 1),), 1)
    value = depth_conv_all(deep, depth_w, zs)
    factor = silu_slope(value) * mask_full[None]

    need = halo_plan(layers, HALO)
    reach = -(-max(need) // height)
    factor_b = factor.astype(jnp.bfloat16)
    blocks = []
    for layer in reversed(range(layers)):
        if layer == layers - 1 or need[layer] != need[layer + 1] - 1:
            blocks.append([])
        blocks[-1].append(layer)
    lows, highs, picks, block_of = {}, {}, {}, {}
    for block, members in enumerate(blocks):
        for layer in members:
            block_of[layer] = block
        for dist in range(1, reach + 1):
            chosen = [layer for layer in members if need[layer] > height * (dist - 1)]
            extra = [grad_out] if block == 0 else []
            if not chosen and not extra:
                continue
            picks[(block, dist)] = chosen
            load = jnp.stack([factor_b[layer] for layer in chosen] + extra)
            lows[(block, dist)] = passed_along(load, "gy", dist)
            highs[(block, dist)] = passed_along(load, "gy", -dist)

    def halo_of(index_of, h, block):
        span = -(-h // height)
        low = [index_of(lows[(block, d)], d) for d in range(span, 0, -1)]
        high = [index_of(highs[(block, d)], d) for d in range(1, span + 1)]
        low = jnp.concatenate(low, axis=1)[:, -h:]
        high = jnp.concatenate(high, axis=1)[:, :h]
        return low, high

    def refreshed(grad, h):
        span = -(-h // height)
        low = jnp.concatenate([passed_along(grad, "gy", d) for d in range(span, 0, -1)], axis=1)
        high = jnp.concatenate([passed_along(grad, "gy", -d) for d in range(1, span + 1)], axis=1)
        return jnp.concatenate([low[:, low.shape[1] - h :], grad, high[:, :h]], axis=1)

    low, high = halo_of(lambda part, d: part[-1], need[layers - 1], 0)
    grad = jnp.concatenate([low, grad_out, high], axis=1)
    plane_list = [None] * layers
    depth_list = [None] * layers
    for layer in reversed(range(layers)):
        h = need[layer]
        if grad.shape[1] != height + 2 * h:
            grad = refreshed(grad, h)
        low, high = halo_of(
            lambda part, d: part[picks[(block_of[layer], d)].index(layer)], h, block_of[layer]
        )
        wide = jnp.concatenate([low.astype(jnp.float32), factor[layer], high.astype(jnp.float32)], axis=1)
        grad_mix = (grad.astype(jnp.float32) * wide).astype(jnp.bfloat16)
        mix_deep = padded_2(grad_mix, (("segment", 0),), 1)
        grad_mid = depth_back(mix_deep, depth_w[layer], zs).astype(jnp.bfloat16)
        rows = grad.shape[1] - 2
        grad = (
            grad[:, 1:-1].astype(jnp.float32) + plane_back(grad_mid, plane_w[layer], rows, width)
        ).astype(jnp.bfloat16)
        depth_list[layer] = grad_mix[:, h : h + height]
        plane_list[layer] = grad_mid[:, h : h + height]

    wide_rows = width_pad(rows_own)

    def kernel_grads(chosen):
        mids = jnp.stack([plane_list[layer] for layer in chosen])
        mixes = jnp.stack([depth_list[layer] for layer in chosen])
        rows = wide_rows[chosen[0] : chosen[-1] + 1]
        shifted = jnp.concatenate(
            [rows[:, :, i : i + height, :, j : j + width] for i in range(3) for j in range(3)],
            axis=3,
        )
        planes = jnp.einsum("lzyox,lzykx->lok", mids, shifted, preferred_element_type=jnp.float32)
        planes = planes.reshape(len(chosen), chans, 9, chans).transpose(0, 2, 1, 3)
        deeps = deep[chosen[0] : chosen[-1] + 1]
        stacked = jnp.concatenate([deeps[:, k : k + zs] for k in range(3)], axis=3)
        depths = jnp.einsum("lzyox,lzykx->lok", mixes, stacked, preferred_element_type=jnp.float32)
        depths = depths.reshape(len(chosen), chans, 3, chans).transpose(0, 2, 1, 3)
        return planes.reshape(len(chosen), -1), depths.reshape(len(chosen), -1)

    first_p, first_d = kernel_grads([0])
    rest_p, rest_d = kernel_grads(list(range(1, layers)))
    planes = jnp.concatenate([first_p, rest_p])
    depths = jnp.concatenate([first_d, rest_d])
    flat = jnp.concatenate([planes, depths], axis=1)
    spread_n = lax.axis_size("gy")
    size = flat.shape[1]
    piece = 128 * -(-size // (128 * spread_n))
    flat = jnp.pad(flat, ((0, 0), (0, piece * spread_n - size))).reshape(layers * spread_n, piece)
    part = lax.all_to_all(flat, ("segment", "gy"), 0, 0, tiled=True).sum(axis=0)
    whole = lax.all_to_all(jnp.broadcast_to(part, (spread_n, piece)), "gy", 0, 0, tiled=True)
    flat = whole.reshape(-1)[:size][None] * scale
    cut = planes.shape[1]
    plane_sum = flat[:, :cut].reshape(-1, 3, 3, chans, chans)
    depth_sum = flat[:, cut:].reshape(-1, 3, chans, chans)
    return (grad, plane_sum, depth_sum)


def solution(mesh):
    placed = (
        P("segment", None, "gy", None, None),
        P("segment", "gy", None, None),
        P("segment", None, None, None, None),
        P("segment", None, None, None),
        P("gy", None),
    )
    return jax.shard_map(
        local,
        mesh=mesh,
        in_specs=placed,
        out_specs=(
            P("segment", "gy", None, None),
            P("segment", None, None, None, None),
            P("segment", None, None, None),
        ),
        check_vma=False,
    )
```

```python
import math

import jax
import jax.numpy as jnp
from jax import lax
from jax.sharding import PartitionSpec as P

TILE = 128
HALO = 4


def padded_2(block, sides, width):
    for axis, dim in sides:
        count = lax.axis_size(axis)
        forward = [(i, i + 1) for i in range(count - 1)]
        backward = [(target, source) for source, target in forward]
        low = lax.ppermute(
            lax.slice_in_dim(block, block.shape[dim] - width, None, axis=dim), axis, forward
        )
        high = lax.ppermute(lax.slice_in_dim(block, 0, width, axis=dim), axis, backward)
        block = jnp.concatenate([low, block, high], axis=dim)
    return block


def passed_along(block, axis, distance):
    devices = range(lax.axis_size(axis))
    route = [(i - distance, i) for i in devices if i - distance in devices]
    return lax.ppermute(block, axis, route)


def halo_plan(layers, depth):
    need = [0] * layers
    left = 0
    for layer in reversed(range(layers)):
        if left == 0:
            left = min(depth, layer + 1)
        need[layer] = left
        left -= 1
    return need


def width_pad(field):
    return jnp.pad(field, [(0, 0)] * (field.ndim - 1) + [(1, 1)])


def plane_conv_all(rows_in, kernel, height, width):
    padded = width_pad(rows_in)
    stacked = jnp.concatenate(
        [padded[:, :, i : i + height, :, j : j + width] for i in range(3) for j in range(3)],
        axis=-2,
    )
    flat = kernel.reshape((kernel.shape[0], 9) + kernel.shape[3:]).transpose(0, 2, 1, 3)
    flat = flat.reshape(kernel.shape[0], kernel.shape[3], -1)
    return jnp.einsum("lok,lzykx->lzyox", flat, stacked, preferred_element_type=jnp.float32)


def depth_conv_all(deep, kernel, depth):
    stacked = jnp.concatenate([deep[:, k : k + depth] for k in range(3)], axis=-2)
    flat = kernel.transpose(0, 2, 1, 3).reshape(kernel.shape[0], kernel.shape[2], -1)
    return jnp.einsum("lok,lzykx->lzyox", flat, stacked, preferred_element_type=jnp.float32)


def plane_back(rows_grad, kernel, height, width):
    padded = width_pad(rows_grad)
    stacked = jnp.concatenate(
        [
            padded[..., 2 - i : 2 - i + height, :, 2 - j : 2 - j + width]
            for i in range(3)
            for j in range(3)
        ],
        axis=-2,
    )
    flat = kernel.reshape(-1, kernel.shape[-1])
    return jnp.einsum("kc,...ykx->...ycx", flat, stacked, preferred_element_type=jnp.float32)


def plane_taps(grad_mid, rows_in, height, width):
    padded = width_pad(rows_in)
    rows_out = []
    for i in range(3):
        row_taps = []
        for j in range(3):
            row_taps.append(
                jnp.einsum(
                    "...yox,...ycx->oc",
                    grad_mid,
                    padded[..., i : i + height, :, j : j + width],
                    preferred_element_type=jnp.float32,
                )
            )
        rows_out.append(jnp.stack(row_taps))
    return jnp.stack(rows_out)


def depth_back(mix_deep, kernel, depth):
    stacked = jnp.concatenate([mix_deep[2 - k : 2 - k + depth] for k in range(3)], axis=-2)
    flat = kernel.reshape(-1, kernel.shape[-1])
    return jnp.einsum("kc,zykx->zycx", flat, stacked, preferred_element_type=jnp.float32)


def depth_taps(grad_mix, deep, depth):
    return jnp.stack(
        [
            jnp.einsum(
                "zyox,zycx->oc", grad_mix, deep[k : k + depth], preferred_element_type=jnp.float32
            )
            for k in range(3)
        ]
    )


def silu_slope(value):
    sig = jax.nn.sigmoid(value)
    return sig * (1.0 + value * (1.0 - sig))


def local(acts, grad_out, w_plane, w_depth, tiles):
    sections = acts.shape[1]
    height = acts.shape[2]
    width = acts.shape[4]
    chans = w_plane.shape[3]
    count = lax.axis_size("segment")
    layers = count * acts.shape[0]
    zs = grad_out.shape[0]
    scale = 1.0 / math.sqrt(sections * height * lax.axis_size("gy") * width)
    segment = lax.axis_index("segment")

    block = acts[0].reshape(count, -1, width)
    kernels = jnp.concatenate(
        [w_plane.reshape(-1, chans, chans), w_depth.reshape(-1, chans, chans)]
    ).reshape(-1, width)
    send = jnp.concatenate([block, jnp.broadcast_to(kernels[None], (count,) + kernels.shape)], axis=1)
    got = lax.all_to_all(send, "segment", 0, 0, tiled=True)
    cut_a = block.shape[1]
    mine = got[:, :cut_a].reshape((count, zs) + acts.shape[2:])
    taps = w_plane.shape[1] * w_plane.shape[2]
    weights = lax.optimization_barrier(got[:, cut_a:].reshape(count, -1, chans, chans))
    plane_w = weights[:, :taps].reshape((count,) + w_plane.shape[1:])
    depth_w = weights[:, taps:].reshape((count,) + w_depth.shape[1:])

    ids = (segment * zs + jnp.arange(zs, dtype=jnp.int32))[:, None] * (width // TILE) + jnp.arange(
        width // TILE, dtype=jnp.int32
    )[None, :]
    hit = jnp.any(tiles[0][None, None, :] == ids[:, :, None], axis=2)
    mask_full = jnp.repeat(hit.astype(jnp.float32), TILE, axis=1)[:, None, None, :]

    rows_own = padded_2(mine, (("gy", 2),), 1)
    mid = plane_conv_all(rows_own, plane_w, height, width).astype(jnp.bfloat16)
    deep = padded_2(mid, (("segment", 1),), 1)
    value = depth_conv_all(deep, depth_w, zs)
    factor = silu_slope(value) * mask_full[None]

    need = halo_plan(layers, HALO)
    reach = -(-max(need) // height)
    factor_b = factor.astype(jnp.bfloat16)
    lows, highs, picks = {}, {}, {}
    for dist in range(1, reach + 1):
        chosen = [layer for layer in range(layers) if need[layer] > height * (dist - 1)]
        picks[dist] = chosen
        load = jnp.stack([factor_b[layer] for layer in chosen] + [grad_out])
        lows[dist] = passed_along(load, "gy", dist)
        highs[dist] = passed_along(load, "gy", -dist)

    def halo_of(index_of, h, own):
        span = -(-h // height)
        low = jnp.concatenate([index_of(lows[d], d) for d in range(span, 0, -1)], axis=1)[:, -h:]
        high = jnp.concatenate([index_of(highs[d], d) for d in range(1, span + 1)], axis=1)[:, :h]
        return low, high

    def refreshed(grad, h):
        span = -(-h // height)
        low = jnp.concatenate([passed_along(grad, "gy", d) for d in range(span, 0, -1)], axis=1)
        high = jnp.concatenate([passed_along(grad, "gy", -d) for d in range(1, span + 1)], axis=1)
        return jnp.concatenate([low[:, low.shape[1] - h :], grad, high[:, :h]], axis=1)

    low, high = halo_of(lambda part, d: part[-1], need[layers - 1], grad_out)
    grad = jnp.concatenate([low, grad_out, high], axis=1)
    plane_list = [None] * layers
    depth_list = [None] * layers
    for layer in reversed(range(layers)):
        h = need[layer]
        if grad.shape[1] != height + 2 * h:
            grad = refreshed(grad, h)
        low, high = halo_of(lambda part, d: part[picks[d].index(layer)], h, None)
        wide = jnp.concatenate([low.astype(jnp.float32), factor[layer], high.astype(jnp.float32)], axis=1)
        grad_mix = (grad.astype(jnp.float32) * wide).astype(jnp.bfloat16)
        mix_deep = padded_2(grad_mix, (("segment", 0),), 1)
        grad_mid = depth_back(mix_deep, depth_w[layer], zs).astype(jnp.bfloat16)
        rows = grad.shape[1] - 2
        grad = (
            grad[:, 1:-1].astype(jnp.float32) + plane_back(grad_mid, plane_w[layer], rows, width)
        ).astype(jnp.bfloat16)
        depth_list[layer] = grad_mix[:, h : h + height]
        plane_list[layer] = grad_mid[:, h : h + height]

    wide_rows = width_pad(rows_own)

    def kernel_grads(chosen):
        mids = jnp.stack([plane_list[layer] for layer in chosen])
        mixes = jnp.stack([depth_list[layer] for layer in chosen])
        rows = wide_rows[chosen[0] : chosen[-1] + 1]
        shifted = jnp.concatenate(
            [rows[:, :, i : i + height, :, j : j + width] for i in range(3) for j in range(3)],
            axis=3,
        )
        planes = jnp.einsum("lzyox,lzykx->lok", mids, shifted, preferred_element_type=jnp.float32)
        planes = planes.reshape(len(chosen), chans, 9, chans).transpose(0, 2, 1, 3)
        deeps = deep[chosen[0] : chosen[-1] + 1]
        stacked = jnp.concatenate([deeps[:, k : k + zs] for k in range(3)], axis=3)
        depths = jnp.einsum("lzyox,lzykx->lok", mixes, stacked, preferred_element_type=jnp.float32)
        depths = depths.reshape(len(chosen), chans, 3, chans).transpose(0, 2, 1, 3)
        return planes.reshape(len(chosen), -1), depths.reshape(len(chosen), -1)

    first_p, first_d = kernel_grads([0])
    rest_p, rest_d = kernel_grads(list(range(1, layers)))
    planes = jnp.concatenate([first_p, rest_p])
    depths = jnp.concatenate([first_d, rest_d])
    flat = jnp.concatenate([planes, depths], axis=1)
    spread_n = lax.axis_size("gy")
    size = flat.shape[1]
    piece = 128 * -(-size // (128 * spread_n))
    flat = jnp.pad(flat, ((0, 0), (0, piece * spread_n - size))).reshape(layers * spread_n, piece)
    part = lax.all_to_all(flat, ("segment", "gy"), 0, 0, tiled=True).sum(axis=0)
    whole = lax.all_to_all(jnp.broadcast_to(part, (spread_n, piece)), "gy", 0, 0, tiled=True)
    flat = whole.reshape(-1)[:size][None] * scale
    cut = planes.shape[1]
    plane_sum = flat[:, :cut].reshape(-1, 3, 3, chans, chans)
    depth_sum = flat[:, cut:].reshape(-1, 3, chans, chans)
    return (grad, plane_sum, depth_sum)


def solution(mesh):
    placed = (
        P("segment", None, "gy", None, None),
        P("segment", "gy", None, None),
        P("segment", None, None, None, None),
        P("segment", None, None, None),
        P("gy", None),
    )
    return jax.shard_map(
        local,
        mesh=mesh,
        in_specs=placed,
        out_specs=(
            P("segment", "gy", None, None),
            P("segment", None, None, None, None),
            P("segment", None, None, None),
        ),
        check_vma=False,
    )
```

```python
import math

import jax
import jax.numpy as jnp
from jax import lax
from jax.sharding import PartitionSpec as P

TILE = 128
HALO = 4


def padded_2(block, sides, width):
    for axis, dim in sides:
        count = lax.axis_size(axis)
        forward = [(i, i + 1) for i in range(count - 1)]
        backward = [(target, source) for source, target in forward]
        low = lax.ppermute(
            lax.slice_in_dim(block, block.shape[dim] - width, None, axis=dim), axis, forward
        )
        high = lax.ppermute(lax.slice_in_dim(block, 0, width, axis=dim), axis, backward)
        block = jnp.concatenate([low, block, high], axis=dim)
    return block


def passed_along(block, axis, distance):
    devices = range(lax.axis_size(axis))
    route = [(i - distance, i) for i in devices if i - distance in devices]
    return lax.ppermute(block, axis, route)


def halo_plan(layers, depth):
    need = [0] * layers
    left = 0
    for layer in reversed(range(layers)):
        if left == 0:
            left = min(depth, layer + 1)
        need[layer] = left
        left -= 1
    return need


def width_pad(field):
    return jnp.pad(field, [(0, 0)] * (field.ndim - 1) + [(1, 1)])


def plane_conv_all(rows_in, kernel, height, width):
    padded = width_pad(rows_in)
    stacked = jnp.concatenate(
        [padded[:, :, i : i + height, :, j : j + width] for i in range(3) for j in range(3)],
        axis=-2,
    )
    flat = kernel.reshape((kernel.shape[0], 9) + kernel.shape[3:]).transpose(0, 2, 1, 3)
    flat = flat.reshape(kernel.shape[0], kernel.shape[3], -1)
    return jnp.einsum("lok,lzykx->lzyox", flat, stacked, preferred_element_type=jnp.float32)


def depth_conv_all(deep, kernel, depth):
    stacked = jnp.concatenate([deep[:, k : k + depth] for k in range(3)], axis=-2)
    flat = kernel.transpose(0, 2, 1, 3).reshape(kernel.shape[0], kernel.shape[2], -1)
    return jnp.einsum("lok,lzykx->lzyox", flat, stacked, preferred_element_type=jnp.float32)


def plane_back(rows_grad, kernel, height, width):
    padded = width_pad(rows_grad)
    stacked = jnp.concatenate(
        [
            padded[..., 2 - i : 2 - i + height, :, 2 - j : 2 - j + width]
            for i in range(3)
            for j in range(3)
        ],
        axis=-2,
    )
    flat = kernel.reshape(-1, kernel.shape[-1])
    return jnp.einsum("kc,...ykx->...ycx", flat, stacked, preferred_element_type=jnp.float32)


def plane_taps(grad_mid, rows_in, height, width):
    padded = width_pad(rows_in)
    rows_out = []
    for i in range(3):
        row_taps = []
        for j in range(3):
            row_taps.append(
                jnp.einsum(
                    "...yox,...ycx->oc",
                    grad_mid,
                    padded[..., i : i + height, :, j : j + width],
                    preferred_element_type=jnp.float32,
                )
            )
        rows_out.append(jnp.stack(row_taps))
    return jnp.stack(rows_out)


def depth_back(mix_deep, kernel, depth):
    stacked = jnp.concatenate([mix_deep[2 - k : 2 - k + depth] for k in range(3)], axis=-2)
    flat = kernel.reshape(-1, kernel.shape[-1])
    return jnp.einsum("kc,zykx->zycx", flat, stacked, preferred_element_type=jnp.float32)


def depth_taps(grad_mix, deep, depth):
    return jnp.stack(
        [
            jnp.einsum(
                "zyox,zycx->oc", grad_mix, deep[k : k + depth], preferred_element_type=jnp.float32
            )
            for k in range(3)
        ]
    )


def silu_slope(value):
    sig = jax.nn.sigmoid(value)
    return sig * (1.0 + value * (1.0 - sig))


def local(acts, grad_out, w_plane, w_depth, tiles):
    sections = acts.shape[1]
    height = acts.shape[2]
    width = acts.shape[4]
    chans = w_plane.shape[3]
    count = lax.axis_size("segment")
    layers = count * acts.shape[0]
    zs = grad_out.shape[0]
    scale = 1.0 / math.sqrt(sections * height * lax.axis_size("gy") * width)
    segment = lax.axis_index("segment")

    block = acts[0].reshape(count, -1, width)
    kernels = jnp.concatenate(
        [w_plane.reshape(-1, chans, chans), w_depth.reshape(-1, chans, chans)]
    ).reshape(-1, width)
    send = jnp.concatenate([block, jnp.broadcast_to(kernels[None], (count,) + kernels.shape)], axis=1)
    got = lax.all_to_all(send, "segment", 0, 0, tiled=True)
    cut_a = block.shape[1]
    mine = got[:, :cut_a].reshape((count, zs) + acts.shape[2:])
    taps = w_plane.shape[1] * w_plane.shape[2]
    weights = lax.optimization_barrier(got[:, cut_a:].reshape(count, -1, chans, chans))
    plane_w = weights[:, :taps].reshape((count,) + w_plane.shape[1:])
    depth_w = weights[:, taps:].reshape((count,) + w_depth.shape[1:])

    ids = (segment * zs + jnp.arange(zs, dtype=jnp.int32))[:, None] * (width // TILE) + jnp.arange(
        width // TILE, dtype=jnp.int32
    )[None, :]
    hit = jnp.any(tiles[0][None, None, :] == ids[:, :, None], axis=2)
    mask_full = jnp.repeat(hit.astype(jnp.float32), TILE, axis=1)[:, None, None, :]

    rows_own = padded_2(mine, (("gy", 2),), 1)
    mid = plane_conv_all(rows_own, plane_w, height, width).astype(jnp.bfloat16)
    deep = padded_2(mid, (("segment", 1),), 1)
    value = depth_conv_all(deep, depth_w, zs)
    factor = silu_slope(value) * mask_full[None]

    need = halo_plan(layers, HALO)
    reach = -(-max(need) // height)
    factor_b = factor.astype(jnp.bfloat16)
    lows, highs, picks = {}, {}, {}
    for dist in range(1, reach + 1):
        chosen = [layer for layer in range(layers) if need[layer] > height * (dist - 1)]
        picks[dist] = chosen
        load = jnp.stack([factor_b[layer] for layer in chosen] + [grad_out])
        lows[dist] = passed_along(load, "gy", dist)
        highs[dist] = passed_along(load, "gy", -dist)

    def halo_of(index_of, h, own):
        span = -(-h // height)
        low = jnp.concatenate([index_of(lows[d], d) for d in range(span, 0, -1)], axis=1)[:, -h:]
        high = jnp.concatenate([index_of(highs[d], d) for d in range(1, span + 1)], axis=1)[:, :h]
        return low, high

    def refreshed(grad, h):
        span = -(-h // height)
        low = jnp.concatenate([passed_along(grad, "gy", d) for d in range(span, 0, -1)], axis=1)
        high = jnp.concatenate([passed_along(grad, "gy", -d) for d in range(1, span + 1)], axis=1)
        return jnp.concatenate([low[:, low.shape[1] - h :], grad, high[:, :h]], axis=1)

    low, high = halo_of(lambda part, d: part[-1], need[layers - 1], grad_out)
    grad = jnp.concatenate([low, grad_out, high], axis=1)
    plane_list = [None] * layers
    depth_list = [None] * layers
    for layer in reversed(range(layers)):
        h = need[layer]
        if grad.shape[1] != height + 2 * h:
            grad = refreshed(grad, h)
        low, high = halo_of(lambda part, d: part[picks[d].index(layer)], h, None)
        wide = jnp.concatenate([low.astype(jnp.float32), factor[layer], high.astype(jnp.float32)], axis=1)
        grad_mix = (grad.astype(jnp.float32) * wide).astype(jnp.bfloat16)
        mix_deep = padded_2(grad_mix, (("segment", 0),), 1)
        grad_mid = depth_back(mix_deep, depth_w[layer], zs).astype(jnp.bfloat16)
        rows = grad.shape[1] - 2
        if layer == 0:
            last = (grad, grad_mid, rows)
        else:
            grad = (
                grad[:, 1:-1].astype(jnp.float32) + plane_back(grad_mid, plane_w[layer], rows, width)
            ).astype(jnp.bfloat16)
        depth_list[layer] = grad_mix[:, h : h + height]
        plane_list[layer] = grad_mid[:, h : h + height]

    wide_rows = width_pad(rows_own)

    def kernel_grads(chosen):
        mids = jnp.stack([plane_list[layer] for layer in chosen])
        mixes = jnp.stack([depth_list[layer] for layer in chosen])
        rows = wide_rows[chosen[0] : chosen[-1] + 1]
        shifted = jnp.concatenate(
            [rows[:, :, i : i + height, :, j : j + width] for i in range(3) for j in range(3)],
            axis=3,
        )
        planes = jnp.einsum("lzyox,lzykx->lok", mids, shifted, preferred_element_type=jnp.float32)
        planes = planes.reshape(len(chosen), chans, 9, chans).transpose(0, 2, 1, 3)
        deeps = deep[chosen[0] : chosen[-1] + 1]
        stacked = jnp.concatenate([deeps[:, k : k + zs] for k in range(3)], axis=3)
        depths = jnp.einsum("lzyox,lzykx->lok", mixes, stacked, preferred_element_type=jnp.float32)
        depths = depths.reshape(len(chosen), chans, 3, chans).transpose(0, 2, 1, 3)
        return planes.reshape(len(chosen), -1), depths.reshape(len(chosen), -1)

    first_p, first_d = kernel_grads([0])
    rest_p, rest_d = kernel_grads(list(range(1, layers)))
    planes = jnp.concatenate([first_p, rest_p])
    depths = jnp.concatenate([first_d, rest_d])
    flat = jnp.concatenate([planes, depths], axis=1)
    spread_n = lax.axis_size("gy")
    size = flat.shape[1]
    piece = 128 * -(-size // (128 * spread_n))
    flat = jnp.pad(flat, ((0, 0), (0, piece * spread_n - size))).reshape(layers * spread_n, piece)
    part = lax.all_to_all(flat, ("segment", "gy"), 0, 0, tiled=True).sum(axis=0)
    grad, grad_mid, rows = last
    part, grad, grad_mid = lax.optimization_barrier((part, grad, grad_mid))
    grad = (
        grad[:, 1:-1].astype(jnp.float32) + plane_back(grad_mid, plane_w[0], rows, width)
    ).astype(jnp.bfloat16)
    whole = lax.all_to_all(jnp.broadcast_to(part, (spread_n, piece)), "gy", 0, 0, tiled=True)
    flat = whole.reshape(-1)[:size][None] * scale
    cut = planes.shape[1]
    plane_sum = flat[:, :cut].reshape(-1, 3, 3, chans, chans)
    depth_sum = flat[:, cut:].reshape(-1, 3, chans, chans)
    return (grad, plane_sum, depth_sum)


def solution(mesh):
    placed = (
        P("segment", None, "gy", None, None),
        P("segment", "gy", None, None),
        P("segment", None, None, None, None),
        P("segment", None, None, None),
        P("gy", None),
    )
    return jax.shard_map(
        local,
        mesh=mesh,
        in_specs=placed,
        out_specs=(
            P("segment", "gy", None, None),
            P("segment", None, None, None, None),
            P("segment", None, None, None),
        ),
        check_vma=False,
    )
```

```python
import math

import jax
import jax.numpy as jnp
from jax import lax
from jax.sharding import PartitionSpec as P

TILE = 128
HALO = 4


def padded_2(block, sides, width):
    for axis, dim in sides:
        count = lax.axis_size(axis)
        forward = [(i, i + 1) for i in range(count - 1)]
        backward = [(target, source) for source, target in forward]
        low = lax.ppermute(
            lax.slice_in_dim(block, block.shape[dim] - width, None, axis=dim), axis, forward
        )
        high = lax.ppermute(lax.slice_in_dim(block, 0, width, axis=dim), axis, backward)
        block = jnp.concatenate([low, block, high], axis=dim)
    return block


def passed_along(block, axis, distance):
    devices = range(lax.axis_size(axis))
    route = [(i - distance, i) for i in devices if i - distance in devices]
    return lax.ppermute(block, axis, route)


def halo_plan(layers, depth):
    need = [0] * layers
    left = 0
    for layer in reversed(range(layers)):
        if left == 0:
            left = min(depth, layer + 1)
        need[layer] = left
        left -= 1
    return need


def width_pad(field):
    return jnp.pad(field, [(0, 0)] * (field.ndim - 1) + [(1, 1)])


def plane_conv_all(rows_in, kernel, height, width):
    padded = width_pad(rows_in)
    stacked = jnp.concatenate(
        [padded[:, :, i : i + height, :, j : j + width] for i in range(3) for j in range(3)],
        axis=-2,
    )
    flat = kernel.reshape((kernel.shape[0], 9) + kernel.shape[3:]).transpose(0, 2, 1, 3)
    flat = flat.reshape(kernel.shape[0], kernel.shape[3], -1)
    return jnp.einsum("lok,lzykx->lzyox", flat, stacked, preferred_element_type=jnp.float32)


def depth_conv_all(deep, kernel, depth):
    stacked = jnp.concatenate([deep[:, k : k + depth] for k in range(3)], axis=-2)
    flat = kernel.transpose(0, 2, 1, 3).reshape(kernel.shape[0], kernel.shape[2], -1)
    return jnp.einsum("lok,lzykx->lzyox", flat, stacked, preferred_element_type=jnp.float32)


def plane_back(rows_grad, kernel, height, width):
    padded = width_pad(rows_grad)
    stacked = jnp.concatenate(
        [
            padded[..., 2 - i : 2 - i + height, :, 2 - j : 2 - j + width]
            for i in range(3)
            for j in range(3)
        ],
        axis=-2,
    )
    flat = kernel.reshape(-1, kernel.shape[-1])
    return jnp.einsum("kc,...ykx->...ycx", flat, stacked, preferred_element_type=jnp.float32)


def plane_taps(grad_mid, rows_in, height, width):
    padded = width_pad(rows_in)
    rows_out = []
    for i in range(3):
        row_taps = []
        for j in range(3):
            row_taps.append(
                jnp.einsum(
                    "...yox,...ycx->oc",
                    grad_mid,
                    padded[..., i : i + height, :, j : j + width],
                    preferred_element_type=jnp.float32,
                )
            )
        rows_out.append(jnp.stack(row_taps))
    return jnp.stack(rows_out)


def depth_back(mix_deep, kernel, depth):
    stacked = jnp.concatenate([mix_deep[2 - k : 2 - k + depth] for k in range(3)], axis=-2)
    flat = kernel.reshape(-1, kernel.shape[-1])
    return jnp.einsum("kc,zykx->zycx", flat, stacked, preferred_element_type=jnp.float32)


def depth_taps(grad_mix, deep, depth):
    return jnp.stack(
        [
            jnp.einsum(
                "zyox,zycx->oc", grad_mix, deep[k : k + depth], preferred_element_type=jnp.float32
            )
            for k in range(3)
        ]
    )


def silu_slope(value):
    sig = jax.nn.sigmoid(value)
    return sig * (1.0 + value * (1.0 - sig))


def local(acts, grad_out, w_plane, w_depth, tiles):
    sections = acts.shape[1]
    height = acts.shape[2]
    width = acts.shape[4]
    chans = w_plane.shape[3]
    count = lax.axis_size("segment")
    layers = count * acts.shape[0]
    zs = grad_out.shape[0]
    scale = 1.0 / math.sqrt(sections * height * lax.axis_size("gy") * width)
    segment = lax.axis_index("segment")

    block = acts[0].reshape(count, -1, width)
    kernels = jnp.concatenate(
        [w_plane.reshape(-1, chans, chans), w_depth.reshape(-1, chans, chans)]
    ).reshape(-1, width)
    send = jnp.concatenate([block, jnp.broadcast_to(kernels[None], (count,) + kernels.shape)], axis=1)
    got = lax.all_to_all(send, "segment", 0, 0, tiled=True)
    cut_a = block.shape[1]
    mine = got[:, :cut_a].reshape((count, zs) + acts.shape[2:])
    taps = w_plane.shape[1] * w_plane.shape[2]
    weights = lax.optimization_barrier(got[:, cut_a:].reshape(count, -1, chans, chans))
    plane_w = weights[:, :taps].reshape((count,) + w_plane.shape[1:])
    depth_w = weights[:, taps:].reshape((count,) + w_depth.shape[1:])

    ids = (segment * zs + jnp.arange(zs, dtype=jnp.int32))[:, None] * (width // TILE) + jnp.arange(
        width // TILE, dtype=jnp.int32
    )[None, :]
    hit = jnp.any(tiles[0][None, None, :] == ids[:, :, None], axis=2)
    mask_full = jnp.repeat(hit.astype(jnp.float32), TILE, axis=1)[:, None, None, :]

    rows_own = padded_2(mine, (("gy", 2),), 1)
    mid = plane_conv_all(rows_own, plane_w, height, width).astype(jnp.bfloat16)
    deep = padded_2(mid, (("segment", 1),), 1)
    value = depth_conv_all(deep, depth_w, zs)
    factor = silu_slope(value) * mask_full[None]

    need = halo_plan(layers, HALO)
    reach = -(-max(need) // height)
    factor_b = factor.astype(jnp.bfloat16)
    lows, highs, picks = {}, {}, {}
    for dist in range(1, reach + 1):
        chosen = [layer for layer in range(layers) if need[layer] > height * (dist - 1)]
        picks[dist] = chosen
        load = jnp.stack([factor_b[layer] for layer in chosen] + [grad_out])
        lows[dist] = passed_along(load, "gy", dist)
        highs[dist] = passed_along(load, "gy", -dist)

    def halo_of(index_of, h, own):
        span = -(-h // height)
        low = jnp.concatenate([index_of(lows[d], d) for d in range(span, 0, -1)], axis=1)[:, -h:]
        high = jnp.concatenate([index_of(highs[d], d) for d in range(1, span + 1)], axis=1)[:, :h]
        return low, high

    def refreshed(grad, h):
        span = -(-h // height)
        low = jnp.concatenate([passed_along(grad, "gy", d) for d in range(span, 0, -1)], axis=1)
        high = jnp.concatenate([passed_along(grad, "gy", -d) for d in range(1, span + 1)], axis=1)
        return jnp.concatenate([low[:, low.shape[1] - h :], grad, high[:, :h]], axis=1)

    low, high = halo_of(lambda part, d: part[-1], need[layers - 1], grad_out)
    grad = jnp.concatenate([low, grad_out, high], axis=1)
    plane_list = [None] * layers
    depth_list = [None] * layers
    for layer in reversed(range(layers)):
        h = need[layer]
        if grad.shape[1] != height + 2 * h:
            grad = refreshed(grad, h)
        low, high = halo_of(lambda part, d: part[picks[d].index(layer)], h, None)
        wide = jnp.concatenate([low.astype(jnp.float32), factor[layer], high.astype(jnp.float32)], axis=1)
        grad_mix = (grad.astype(jnp.float32) * wide).astype(jnp.bfloat16)
        mix_deep = padded_2(grad_mix, (("segment", 0),), 1)
        grad_mid = depth_back(mix_deep, depth_w[layer], zs).astype(jnp.bfloat16)
        rows = grad.shape[1] - 2
        grad = (
            grad[:, 1:-1].astype(jnp.float32) + plane_back(grad_mid, plane_w[layer], rows, width)
        ).astype(jnp.bfloat16)
        depth_list[layer] = grad_mix[:, h : h + height]
        plane_list[layer] = grad_mid[:, h : h + height]

    wide_rows = width_pad(rows_own)

    def kernel_grads(chosen):
        mids = jnp.stack([plane_list[layer] for layer in chosen])
        mixes = jnp.stack([depth_list[layer] for layer in chosen])
        rows = wide_rows[chosen[0] : chosen[-1] + 1]
        shifted = jnp.concatenate(
            [rows[:, :, i : i + height, :, j : j + width] for i in range(3) for j in range(3)],
            axis=3,
        )
        planes = jnp.einsum("lzyox,lzykx->lok", mids, shifted, preferred_element_type=jnp.float32)
        planes = planes.reshape(len(chosen), chans, 9, chans).transpose(0, 2, 1, 3)
        deeps = deep[chosen[0] : chosen[-1] + 1]
        stacked = jnp.concatenate([deeps[:, k : k + zs] for k in range(3)], axis=3)
        depths = jnp.einsum("lzyox,lzykx->lok", mixes, stacked, preferred_element_type=jnp.float32)
        depths = depths.reshape(len(chosen), chans, 3, chans).transpose(0, 2, 1, 3)
        return planes.reshape(len(chosen), -1), depths.reshape(len(chosen), -1)

    first_p, first_d = kernel_grads([0, 1])
    rest_p, rest_d = kernel_grads(list(range(2, layers)))
    planes = jnp.concatenate([first_p, rest_p])
    depths = jnp.concatenate([first_d, rest_d])
    flat = jnp.concatenate([planes, depths], axis=1)
    spread_n = lax.axis_size("gy")
    size = flat.shape[1]
    piece = 128 * -(-size // (128 * spread_n))
    flat = jnp.pad(flat, ((0, 0), (0, piece * spread_n - size))).reshape(layers * spread_n, piece)
    part = lax.all_to_all(flat, ("segment", "gy"), 0, 0, tiled=True).sum(axis=0)
    whole = lax.all_to_all(jnp.broadcast_to(part, (spread_n, piece)), "gy", 0, 0, tiled=True)
    flat = whole.reshape(-1)[:size][None] * scale
    cut = planes.shape[1]
    plane_sum = flat[:, :cut].reshape(-1, 3, 3, chans, chans)
    depth_sum = flat[:, cut:].reshape(-1, 3, chans, chans)
    return (grad, plane_sum, depth_sum)


def solution(mesh):
    placed = (
        P("segment", None, "gy", None, None),
        P("segment", "gy", None, None),
        P("segment", None, None, None, None),
        P("segment", None, None, None),
        P("gy", None),
    )
    return jax.shard_map(
        local,
        mesh=mesh,
        in_specs=placed,
        out_specs=(
            P("segment", "gy", None, None),
            P("segment", None, None, None, None),
            P("segment", None, None, None),
        ),
        check_vma=False,
    )
```
